128 devices in a mesh: seq: 32 (over x, y, core), fsdp: 4 (over z).
Axes of the slice: x: 4, y: 4, z: 4, core: 2. Of those that a mesh axis runs over, the one named last changes fastest.
Arguments:
- patches: bfloat16 [32768, 1280], P(('seq', 'fsdp')), may hold values from -6 to 6
- vis_index: int32 [32768], P(('seq', 'fsdp')), may hold values from 0 to 131071, as said below
- kv_list: int32 [256, 16], P(('seq', 'fsdp')), may hold values from 0 to 255, as said below
- kv_count: int32 [256], P(('seq', 'fsdp')), may hold values from 1 to 16, as said below
- global_tiles: int32 [2], replicated, may hold values from 0 to 255
- frame_table: bfloat16 [256, 1280], replicated, may hold values from -3 to 3
- space_table: bfloat16 [512, 1280], replicated, may hold values from -3 to 3
- ln_gain: bfloat16 [1280], replicated, may hold values from 0.25 to 1.75
- ln_bias: bfloat16 [1280], replicated, may hold values from -3 to 3
- w_qkv: bfloat16 [1280, 3840], P('fsdp')
- w_out: bfloat16 [1280, 1280], P('fsdp'), may hold values from -1.25 to 1.25
Outputs:
- attended: bfloat16 [32768, 1280], P(('seq', 'fsdp'))
The draws below stay inside these ranges and needn't reach their ends.
Inputs may be any that keep to these rules, and one draw needn't show every extreme that they name: `vis_index`: exactly one visible position in each aligned group of four; strictly increasing. `kv_list`: the first entry of query tile i is i itself; entries may repeat; every entry t satisfies |t // 8 - i // 8| <= 2. Over all entries of an aligned run of 2 query tiles, the tiles that lie in any one group other than the run's own group (group = tile // 8) number at most 3 distinct ones, and exactly 3 for every such group within two of the run's own. On every device at least one query tile has kv_count = 16.
All inputs are finite; a program needn't handle non-finite values.
Results may differ from the reference program's by a relative error of at most 0.0065.
Values may be sent and summed in bfloat16 or wider, within the bound.
No kernel may reach another device: no remote copies, remote signals or barrier semaphores. Data moves between devices by JAX's collectives and lax.ppermute only.
A program may use at most 192 MiB of HBM per device.

```python
import jax
import jax.numpy as jnp
from jax import lax

D = 1280
HEADS = 16
HEAD_DIM = 80
TILE = 128
KT = 16
GLOBAL = 2
NEAR_TILES = 3
PATCHES = 512
VIS = 32768
QTILES = 256
TILES_DEV = 2
GROUP_TILES = 8
FRAMES = 256


def draw_vis_index(key, part):
    positions = jnp.arange(VIS, dtype=jnp.int32)
    choose = jax.random.randint(jax.random.fold_in(key, 21), (VIS,), 0, 4, dtype=jnp.int32)
    choose = jnp.where(positions == 0, 0, choose)
    choose = jnp.where(positions == VIS - 1, 3, choose)
    return (4 * positions + choose).astype(jnp.int32)


def draw_kv_list(key, part):
    dev_count = QTILES // TILES_DEV
    group_count = QTILES // GROUP_TILES
    tiles_all = jnp.arange(QTILES, dtype=jnp.int32)
    dev_ids = tiles_all // TILES_DEV
    own_group = tiles_all // GROUP_TILES
    offsets = jnp.array([-2, -1, 1, 2], dtype=jnp.int32)
    pos_noise = jax.random.randint(jax.random.fold_in(key, 25), (dev_count, 4, GROUP_TILES), 0, 1 << 20, dtype=jnp.int32) * 64 + jnp.arange(GROUP_TILES, dtype=jnp.int32)
    unused, near_pos = lax.top_k(pos_noise, NEAR_TILES)
    near_pos = near_pos.astype(jnp.int32)[dev_ids]
    near_group = own_group[:, None, None] + offsets[None, :, None]
    foreign = (near_group * GROUP_TILES + near_pos).reshape(QTILES, 4 * NEAR_TILES)
    foreign_ok = jnp.broadcast_to((near_group >= 0) & (near_group < group_count), (QTILES, 4, NEAR_TILES)).reshape(QTILES, 4 * NEAR_TILES)
    own_tiles = own_group[:, None] * GROUP_TILES + jnp.arange(GROUP_TILES, dtype=jnp.int32)[None, :]
    pool_tiles = jnp.concatenate([own_tiles, foreign], axis=1).astype(jnp.int32)
    pool_ok = jnp.concatenate([jnp.ones((QTILES, GROUP_TILES), dtype=bool), foreign_ok], axis=1)
    pool_size = GROUP_TILES + 4 * NEAR_TILES
    pool_ids = jnp.arange(pool_size, dtype=jnp.int32)
    pick_noise = jax.random.randint(jax.random.fold_in(key, 26), (QTILES, KT, pool_size), 0, 1 << 20, dtype=jnp.int32) * 256 + pool_ids
    pick_noise = jnp.where(pool_ok[:, None, :], pick_noise, -1 - pool_ids)
    unused2, picked = lax.top_k(pick_noise, 1)
    random_fill = jnp.take_along_axis(pool_tiles, picked[:, :, 0].astype(jnp.int32), axis=1)
    host_slot = jax.random.randint(jax.random.fold_in(key, 27), (dev_count,), 0, TILES_DEV, dtype=jnp.int32)[dev_ids]
    is_host = tiles_all % TILES_DEV == host_slot
    slot_ids = jnp.arange(KT, dtype=jnp.int32)
    foreign_slot = jnp.clip(slot_ids - 1, 0, 4 * NEAR_TILES - 1)
    foreign_at = foreign[:, foreign_slot]
    ok_at = foreign_ok[:, foreign_slot]
    use_foreign = is_host[:, None] & (slot_ids >= 1)[None, :] & (slot_ids <= 4 * NEAR_TILES)[None, :] & ok_at
    body_list = jnp.where(use_foreign, foreign_at, random_fill).astype(jnp.int32)
    order_noise = jax.random.randint(jax.random.fold_in(key, 28), (QTILES, KT), 0, 1 << 20, dtype=jnp.int32) * 256 + slot_ids
    order_noise = jnp.where(slot_ids[None, :] == 0, -1, order_noise)
    slot_order = jnp.argsort(order_noise, axis=1, stable=True).astype(jnp.int32)
    shuffled = jnp.take_along_axis(body_list, slot_order, axis=1)
    return jnp.where(slot_ids[None, :] == 0, tiles_all[:, None], shuffled).astype(jnp.int32)


def draw_kv_count(key, part):
    counts = jax.random.randint(jax.random.fold_in(key, 23), (QTILES,), 1, KT + 1, dtype=jnp.int32)
    full_slot = jax.random.randint(jax.random.fold_in(key, 24), (QTILES // TILES_DEV,), 0, TILES_DEV, dtype=jnp.int32)
    tiles_all = jnp.arange(QTILES, dtype=jnp.int32)
    is_full = tiles_all % TILES_DEV == jnp.repeat(full_slot, TILES_DEV)
    return jnp.where(is_full, KT, counts).astype(jnp.int32)


def draw_w_qkv(key, part):
    scale = D ** (-0.5)
    whole = jax.random.normal(jax.random.fold_in(key, 35), (D, 3 * D), jnp.float32) * scale
    return whole.astype(jnp.bfloat16)


def steps_of(stream_key, shape, split, smallest, high):
    def one(axis_at, blocks):
        heights = jax.random.uniform(jax.random.fold_in(jax.random.fold_in(stream_key, 6), axis_at), (blocks,), jnp.float32, smallest / len(split), high / len(split))
        return jnp.repeat(jnp.exp(heights), shape[axis_at] // blocks).reshape((-1,) + (1,) * (len(shape) - axis_at - 1))

    gain = one(*split[0])
    for cut in split[1:]:
        gain = gain * one(*cut)
    return gain


def scatter_about(rng, shape, width, most, shards=(), held_as=jnp.bfloat16):
    gain = steps_of(rng, shape, shards, -0.22, 0.18) if shards else 1.0
    values = jax.random.normal(rng, shape, jnp.float32) * width * gain
    return jnp.minimum(jnp.maximum(values, -most), most).astype(held_as)


def setup_inputs(seed: int = 0) -> dict:
    key_of = jax.random.split(jax.random.key(seed), 12)
    return {
        "patches": scatter_about(key_of[0], (VIS, D), 1.0, 6.0, ((0, 128),)),
        "vis_index": draw_vis_index(jax.random.fold_in(key_of[11], 71), 0),
        "kv_list": draw_kv_list(jax.random.fold_in(key_of[11], 71), 0),
        "kv_count": draw_kv_count(jax.random.fold_in(key_of[11], 71), 0),
        "global_tiles": jax.random.randint(key_of[4], (GLOBAL,), 0, QTILES).astype(jnp.int32),
        "frame_table": scatter_about(key_of[5], (FRAMES, D), 0.5, 3.0),
        "space_table": scatter_about(key_of[6], (PATCHES, D), 0.5, 3.0),
        "ln_gain": jnp.clip(1.0 + 0.15 * jax.random.normal(key_of[7], (D,), jnp.float32), 0.25, 1.75).astype(jnp.bfloat16),
        "ln_bias": scatter_about(key_of[8], (D,), 0.5, 3.0),
        "w_qkv": draw_w_qkv(jax.random.fold_in(key_of[11], 71), 0),
        "w_out": scatter_about(key_of[10], (D, D), (D // 64) ** -0.5, 1.25, ((0, 4),)),
    }


def layer_norm(stream, ln_gain, ln_bias):
    stream32 = stream.astype(jnp.float32)
    mean_val = lax.optimization_barrier(jnp.mean(stream32, axis=-1, keepdims=True))
    centred = stream32 - mean_val
    variance = lax.optimization_barrier(jnp.mean(centred * centred, axis=-1, keepdims=True))
    scaled = centred * lax.rsqrt(variance + 1e-06)
    return (scaled * ln_gain.astype(jnp.float32) + ln_bias.astype(jnp.float32)).astype(jnp.bfloat16)

def attend_tile(query_tile, key_values, key_live):
    key_rows = key_values.shape[0]
    queries_h = query_tile.reshape(TILE, HEADS, HEAD_DIM).astype(jnp.float32)
    keys_h = key_values[:, :D].reshape(key_rows, HEADS, HEAD_DIM).astype(jnp.float32)
    values_h = key_values[:, D:].reshape(key_rows, HEADS, HEAD_DIM).astype(jnp.float32)
    scores = jnp.einsum('qhd,khd->hqk', queries_h, keys_h) * HEAD_DIM ** (-0.5)
    scores = jnp.where(key_live[None, None, :], scores, -jnp.inf)
    row_max = lax.optimization_barrier(jnp.max(scores, axis=-1, keepdims=True))
    weights_raw = jnp.exp(scores - row_max)
    probs = (weights_raw / lax.optimization_barrier(jnp.sum(weights_raw, axis=-1, keepdims=True))).astype(jnp.bfloat16)
    mixed_h = jnp.einsum('hqk,khd->qhd', probs.astype(jnp.float32), values_h)
    return mixed_h.reshape(TILE, D).astype(jnp.bfloat16)

def reference(patches, vis_index, kv_list, kv_count, global_tiles, frame_table, space_table, ln_gain, ln_bias, w_qkv, w_out):
    frame_ids = vis_index // PATCHES
    patch_ids = vis_index % PATCHES
    stream = (patches.astype(jnp.float32) + frame_table[frame_ids].astype(jnp.float32) + space_table[patch_ids].astype(jnp.float32)).astype(jnp.bfloat16)
    normed = layer_norm(stream, ln_gain, ln_bias)
    qkv = jnp.dot(normed, w_qkv, preferred_element_type=jnp.float32).astype(jnp.bfloat16)
    query = qkv[:, :D].reshape(QTILES, TILE, D)
    kv_tiles = qkv[:, D:].reshape(QTILES, TILE, 2 * D)
    global_kv = kv_tiles[global_tiles]

    def per_tile(tile_args):
        query_tile, tile_list, live_count = tile_args
        slot_live = jnp.concatenate([jnp.arange(KT) < live_count, jnp.ones((GLOBAL,), dtype=bool)])
        key_live = jnp.repeat(slot_live, TILE)
        key_values = jnp.concatenate([kv_tiles[tile_list], global_kv], axis=0).reshape((KT + GLOBAL) * TILE, 2 * D)
        return attend_tile(query_tile, key_values, key_live)
    heads_out = lax.map(per_tile, (query, kv_list, kv_count)).reshape(VIS, D)
    return jnp.dot(heads_out, w_out, preferred_element_type=jnp.float32).astype(jnp.bfloat16)
```

```python
import jax
import jax.numpy as jnp
from jax import lax
from jax.sharding import PartitionSpec as P

HEADS = 16
TILE = 128
KT = 16
GLOBAL = 2
PATCHES = 512
NEAR = 3
REACH = (-2, -1, 1, 2)


def passed_along(block, axis, distance):
    devices = range(lax.axis_size(axis))
    route = [(i - distance, i) for i in devices if i - distance in devices]
    return lax.ppermute(block, axis, route)


def layer_norm(stream, ln_gain, ln_bias):
    stream32 = stream.astype(jnp.float32)
    mean_val = jnp.mean(stream32, axis=-1, keepdims=True)
    centred = stream32 - mean_val
    variance = jnp.mean(centred * centred, axis=-1, keepdims=True)
    scaled = centred * lax.rsqrt(variance + 1e-06)
    return (scaled * ln_gain.astype(jnp.float32) + ln_bias.astype(jnp.float32)).astype(jnp.bfloat16)


def embed(patches, vis_index, frame_table, space_table):
    frame_ids = vis_index // PATCHES
    patch_ids = vis_index % PATCHES
    return (
        patches.astype(jnp.float32)
        + frame_table[frame_ids].astype(jnp.float32)
        + space_table[patch_ids].astype(jnp.float32)
    ).astype(jnp.bfloat16)


def near_tiles(entries, group, group_tiles):
    cand = group * group_tiles + jnp.arange(group_tiles, dtype=jnp.int32)
    named = jnp.any(entries.reshape(-1, 1) == cand[None, :], axis=0)
    rank = jnp.cumsum(named.astype(jnp.int32)) - 1
    local_ids = jnp.arange(group_tiles, dtype=jnp.int32)
    picks = jnp.stack(
        [jnp.sum(jnp.where(named & (rank == j), local_ids, 0)) for j in range(NEAR)]
    )
    return picks, rank


def attend_tile(query_tile, key_values, key_live, feat_width):
    head_size = feat_width // HEADS
    key_rows = key_values.shape[0]
    queries_h = query_tile.reshape(TILE, HEADS, head_size)
    keys_h = key_values[:, :feat_width].reshape(key_rows, HEADS, head_size)
    values_h = key_values[:, feat_width:].reshape(key_rows, HEADS, head_size)
    scores = jnp.einsum(
        "qhd,khd->hqk", queries_h, keys_h, preferred_element_type=jnp.float32
    ) * head_size ** (-0.5)
    scores = jnp.where(key_live[None, None, :], scores, -jnp.inf)
    row_max = jnp.max(scores, axis=-1, keepdims=True)
    weights_raw = jnp.exp(scores - row_max)
    probs = (weights_raw / jnp.sum(weights_raw, axis=-1, keepdims=True)).astype(jnp.bfloat16)
    mixed_h = jnp.einsum("hqk,khd->qhd", probs, values_h, preferred_element_type=jnp.float32)
    return mixed_h.reshape(TILE, feat_width).astype(jnp.bfloat16)


def local(
    patches,
    vis_index,
    kv_list,
    kv_count,
    global_tiles,
    frame_table,
    space_table,
    ln_gain,
    ln_bias,
    w_qkv,
    w_out,
):
    tok_rows = patches.shape[0]
    feat_width = patches.shape[1]
    tile_count = tok_rows // TILE
    fsdp_size = lax.axis_size("fsdp")
    seq_size = lax.axis_size("seq")
    seq_at = lax.axis_index("seq")
    dev_at = seq_at * fsdp_size + lax.axis_index("fsdp")
    group_tiles = tile_count * fsdp_size

    stream = embed(patches, vis_index, frame_table, space_table)

    global_rows = []
    for slot_no in range(GLOBAL):
        tile_id = global_tiles[slot_no]
        mine = tile_id // tile_count == dev_at
        rows = lax.dynamic_slice_in_dim(stream, tile_id % tile_count * TILE, TILE, 0)
        global_rows.append(jnp.where(mine, rows, jnp.zeros_like(rows)))
    global_stream = lax.psum(jnp.concatenate(global_rows, axis=0), ("seq", "fsdp"))

    w_full = lax.all_gather(w_qkv, "fsdp", axis=0, tiled=True)
    normed = layer_norm(stream, ln_gain, ln_bias)
    qkv = jnp.dot(normed, w_full, preferred_element_type=jnp.float32).astype(jnp.bfloat16)
    query = qkv[:, :feat_width]
    keyval = qkv[:, feat_width:]
    global_normed = layer_norm(global_stream, ln_gain, ln_bias)
    global_kv = jnp.dot(
        global_normed, w_full[:, feat_width:], preferred_element_type=jnp.float32
    ).astype(jnp.bfloat16).reshape(GLOBAL, TILE, 2 * feat_width)

    group_block = lax.all_gather(keyval, "fsdp", axis=0, tiled=True).reshape(
        group_tiles, TILE, 2 * feat_width
    )
    seq_lists = lax.all_gather(kv_list, "seq", axis=0, tiled=True)

    near_blocks = []
    near_rank = []
    for reach in REACH:
        distance = -reach
        dest = jnp.clip(seq_at + distance, 0, seq_size - 1)
        dest_lists = lax.dynamic_slice_in_dim(seq_lists, dest * tile_count, tile_count, 0)
        send_ids, unused = near_tiles(dest_lists, seq_at, group_tiles)
        sent = passed_along(group_block[send_ids], "seq", distance)
        near_blocks.append(sent)
        unused2, rank = near_tiles(kv_list, seq_at + reach, group_tiles)
        near_rank.append(rank)
    window = jnp.concatenate([group_block] + near_blocks + [global_kv], axis=0)
    near_rank = jnp.stack(near_rank)

    entry_group = kv_list // group_tiles
    entry_local = kv_list % group_tiles
    reach_of = entry_group - seq_at
    reach_slot = jnp.where(reach_of < 0, reach_of + 2, reach_of + 1)
    reach_slot = jnp.clip(reach_slot, 0, len(REACH) - 1)
    entry_rank = near_rank[reach_slot, entry_local]
    local_lists = jnp.where(
        reach_of == 0, entry_local, group_tiles + NEAR * reach_slot + entry_rank
    )
    global_slots = group_tiles + NEAR * len(REACH) + jnp.arange(GLOBAL, dtype=jnp.int32)

    query_tiles = query.reshape(tile_count, TILE, feat_width)

    def per_tile(tile_args):
        query_tile, local_ids, live_count = tile_args
        slot_live_row = jnp.concatenate(
            [jnp.arange(KT) < live_count, jnp.ones((GLOBAL,), dtype=bool)]
        )
        key_live = jnp.repeat(slot_live_row, TILE)
        key_values = window[jnp.concatenate([local_ids, global_slots])].reshape(
            (KT + GLOBAL) * TILE, 2 * feat_width
        )
        return attend_tile(query_tile, key_values, key_live, feat_width)

    heads_out = lax.map(per_tile, (query_tiles, local_lists, kv_count)).reshape(
        tok_rows, feat_width
    )
    return jnp.dot(
        heads_out,
        lax.all_gather(w_out, "fsdp", axis=0, tiled=True),
        preferred_element_type=jnp.float32,
    ).astype(jnp.bfloat16)


def solution(mesh):
    return jax.shard_map(
        local,
        mesh=mesh,
        in_specs=(
            P(("seq", "fsdp"), None),
            P(("seq", "fsdp")),
            P(("seq", "fsdp"), None),
            P(("seq", "fsdp")),
            P(),
            P(),
            P(),
            P(),
            P(),
            P("fsdp", None),
            P("fsdp", None),
        ),
        out_specs=P(("seq", "fsdp"), None),
        check_vma=False,
    )
```

```python
import jax
import jax.numpy as jnp
from jax import lax
from jax.sharding import PartitionSpec as P

HEADS = 16
TILE = 128
KT = 16
GLOBAL = 2
PATCHES = 512
NEAR = 3
REACH = (-2, -1, 1, 2)


def passed_along(block, axis, distance):
    devices = range(lax.axis_size(axis))
    route = [(i - distance, i) for i in devices if i - distance in devices]
    return lax.ppermute(block, axis, route)


def layer_norm(stream, ln_gain, ln_bias):
    stream32 = stream.astype(jnp.float32)
    mean_val = jnp.mean(stream32, axis=-1, keepdims=True)
    centred = stream32 - mean_val
    variance = jnp.mean(centred * centred, axis=-1, keepdims=True)
    scaled = centred * lax.rsqrt(variance + 1e-06)
    return (scaled * ln_gain.astype(jnp.float32) + ln_bias.astype(jnp.float32)).astype(jnp.bfloat16)


def embed(patches, vis_index, frame_table, space_table):
    frame_ids = vis_index // PATCHES
    patch_ids = vis_index % PATCHES
    return (
        patches.astype(jnp.float32)
        + frame_table[frame_ids].astype(jnp.float32)
        + space_table[patch_ids].astype(jnp.float32)
    ).astype(jnp.bfloat16)


def near_tiles(entries, group, group_tiles):
    cand = group * group_tiles + jnp.arange(group_tiles, dtype=jnp.int32)
    named = jnp.any(entries.reshape(-1, 1) == cand[None, :], axis=0)
    rank = jnp.cumsum(named.astype(jnp.int32)) - 1
    local_ids = jnp.arange(group_tiles, dtype=jnp.int32)
    picks = jnp.stack(
        [jnp.sum(jnp.where(named & (rank == j), local_ids, 0)) for j in range(NEAR)]
    )
    return picks, rank


def attend_tile(query_tile, key_values, key_live, feat_width):
    head_size = feat_width // HEADS
    key_rows = key_values.shape[0]
    queries_h = query_tile.reshape(TILE, HEADS, head_size)
    keys_h = key_values[:, :feat_width].reshape(key_rows, HEADS, head_size)
    values_h = key_values[:, feat_width:].reshape(key_rows, HEADS, head_size)
    scores = jnp.einsum(
        "qhd,khd->hqk", queries_h, keys_h, preferred_element_type=jnp.float32
    ) * head_size ** (-0.5)
    scores = jnp.where(key_live[None, None, :], scores, -jnp.inf)
    row_max = jnp.max(scores, axis=-1, keepdims=True)
    weights_raw = jnp.exp(scores - row_max)
    probs = (weights_raw / jnp.sum(weights_raw, axis=-1, keepdims=True)).astype(jnp.bfloat16)
    mixed_h = jnp.einsum("hqk,khd->qhd", probs, values_h, preferred_element_type=jnp.float32)
    return mixed_h.reshape(TILE, feat_width).astype(jnp.bfloat16)


def local(
    patches,
    vis_index,
    kv_list,
    kv_count,
    global_tiles,
    frame_table,
    space_table,
    ln_gain,
    ln_bias,
    w_qkv,
    w_out,
):
    tok_rows = patches.shape[0]
    feat_width = patches.shape[1]
    tile_count = tok_rows // TILE
    fsdp_size = lax.axis_size("fsdp")
    seq_size = lax.axis_size("seq")
    seq_at = lax.axis_index("seq")
    dev_at = seq_at * fsdp_size + lax.axis_index("fsdp")
    group_tiles = tile_count * fsdp_size

    stream = embed(patches, vis_index, frame_table, space_table)

    dev_count = seq_size * fsdp_size
    global_rows = []
    owners = []
    for slot_no in range(GLOBAL):
        tile_id = global_tiles[slot_no]
        owners.append(tile_id // tile_count)
        global_rows.append(
            lax.dynamic_slice_in_dim(stream, tile_id % tile_count * TILE, TILE, 0)
        )
    global_stream = jnp.stack(global_rows)
    owners = jnp.stack(owners)
    bit_order = sorted(range(dev_count.bit_length() - 1), key=lambda b: -b)
    done_bits = 0
    for bit in bit_order:
        step = 1 << bit
        held = ((dev_at ^ owners) & ~done_bits) == 0
        got = lax.ppermute(
            global_stream, ("seq", "fsdp"), [(i, i ^ step) for i in range(dev_count)]
        )
        global_stream = jnp.where(held[:, None, None], global_stream, got)
        done_bits |= step
    global_stream = global_stream.reshape(GLOBAL * TILE, feat_width)

    w_full = lax.all_gather(w_qkv, "fsdp", axis=0, tiled=True)
    normed = layer_norm(stream, ln_gain, ln_bias)
    qkv = jnp.dot(normed, w_full, preferred_element_type=jnp.float32).astype(jnp.bfloat16)
    query = qkv[:, :feat_width]
    keyval = qkv[:, feat_width:]
    global_normed = layer_norm(global_stream, ln_gain, ln_bias)
    global_kv = jnp.dot(
        global_normed, w_full[:, feat_width:], preferred_element_type=jnp.float32
    ).astype(jnp.bfloat16).reshape(GLOBAL, TILE, 2 * feat_width)

    group_block = lax.all_gather(keyval, "fsdp", axis=0, tiled=True).reshape(
        group_tiles, TILE, 2 * feat_width
    )
    near_blocks = []
    near_rank = []
    for reach in REACH:
        picks, rank = near_tiles(kv_list, seq_at + reach, group_tiles)
        asked = passed_along(picks, "seq", reach)
        near_blocks.append(passed_along(group_block[asked], "seq", -reach))
        near_rank.append(rank)
    window = jnp.concatenate([group_block] + near_blocks + [global_kv], axis=0)
    near_rank = jnp.stack(near_rank)

    entry_group = kv_list // group_tiles
    entry_local = kv_list % group_tiles
    reach_of = entry_group - seq_at
    reach_slot = jnp.where(reach_of < 0, reach_of + 2, reach_of + 1)
    reach_slot = jnp.clip(reach_slot, 0, len(REACH) - 1)
    entry_rank = near_rank[reach_slot, entry_local]
    local_lists = jnp.where(
        reach_of == 0, entry_local, group_tiles + NEAR * reach_slot + entry_rank
    )
    global_slots = group_tiles + NEAR * len(REACH) + jnp.arange(GLOBAL, dtype=jnp.int32)

    query_tiles = query.reshape(tile_count, TILE, feat_width)

    def per_tile(tile_args):
        query_tile, local_ids, live_count = tile_args
        slot_live_row = jnp.concatenate(
            [jnp.arange(KT) < live_count, jnp.ones((GLOBAL,), dtype=bool)]
        )
        key_live = jnp.repeat(slot_live_row, TILE)
        key_values = window[jnp.concatenate([local_ids, global_slots])].reshape(
            (KT + GLOBAL) * TILE, 2 * feat_width
        )
        return attend_tile(query_tile, key_values, key_live, feat_width)

    heads_out = lax.map(per_tile, (query_tiles, local_lists, kv_count)).reshape(
        tok_rows, feat_width
    )
    return jnp.dot(
        heads_out,
        lax.all_gather(w_out, "fsdp", axis=0, tiled=True),
        preferred_element_type=jnp.float32,
    ).astype(jnp.bfloat16)


def solution(mesh):
    return jax.shard_map(
        local,
        mesh=mesh,
        in_specs=(
            P(("seq", "fsdp"), None),
            P(("seq", "fsdp")),
            P(("seq", "fsdp"), None),
            P(("seq", "fsdp")),
            P(),
            P(),
            P(),
            P(),
            P(),
            P("fsdp", None),
            P("fsdp", None),
        ),
        out_specs=P(("seq", "fsdp"), None),
        check_vma=False,
    )
```

```python
import jax
import jax.numpy as jnp
from jax import lax
from jax.experimental import pallas as pl
from jax.experimental.pallas import tpu as pltpu
from jax.sharding import PartitionSpec as P

HEADS = 16
TILE = 128
KT = 16
GLOBAL = 2
PATCHES = 512
NEAR = 3
REACH = (-2, -1, 1, 2)


def passed_along(block, axis, distance):
    devices = range(lax.axis_size(axis))
    route = [(i - distance, i) for i in devices if i - distance in devices]
    return lax.ppermute(block, axis, route)


def layer_norm(stream, ln_gain, ln_bias):
    stream32 = stream.astype(jnp.float32)
    mean_val = jnp.mean(stream32, axis=-1, keepdims=True)
    centred = stream32 - mean_val
    variance = jnp.mean(centred * centred, axis=-1, keepdims=True)
    scaled = centred * lax.rsqrt(variance + 1e-06)
    return (scaled * ln_gain.astype(jnp.float32) + ln_bias.astype(jnp.float32)).astype(jnp.bfloat16)


def embed(patches, vis_index, frame_table, space_table):
    frame_ids = vis_index // PATCHES
    patch_ids = vis_index % PATCHES
    return (
        patches.astype(jnp.float32)
        + frame_table[frame_ids].astype(jnp.float32)
        + space_table[patch_ids].astype(jnp.float32)
    ).astype(jnp.bfloat16)


def near_tiles(entries, group, group_tiles):
    cand = group * group_tiles + jnp.arange(group_tiles, dtype=jnp.int32)
    named = jnp.any(entries.reshape(-1, 1) == cand[None, :], axis=0)
    rank = jnp.cumsum(named.astype(jnp.int32)) - 1
    local_ids = jnp.arange(group_tiles, dtype=jnp.int32)
    picks = jnp.stack(
        [jnp.sum(jnp.where(named & (rank == j), local_ids, 0)) for j in range(NEAR)]
    )
    return picks, rank


def attention_kernel(slots_ref, counts_ref, q_ref, kv_ref, o_ref, s_scr, v_scr):
    tile_at = pl.program_id(0)
    slot_at = pl.program_id(1)
    slot_count = KT + GLOBAL
    feat_width = q_ref.shape[-1]
    head_size = feat_width // HEADS
    live_count = counts_ref[tile_at]
    live = (slot_at >= KT) | (slot_at < live_count)
    key_at = pl.multiple_of(slot_at * TILE, TILE)

    @pl.when(live)
    def _():
        for head in range(HEADS):
            cols = slice(head * head_size, (head + 1) * head_size)
            scores = lax.dot_general(
                q_ref[0, :, cols], kv_ref[0, :, cols], (((1,), (1,)), ((), ())),
                preferred_element_type=jnp.float32,
            )
            s_scr[head, :, pl.ds(key_at, TILE)] = scores * head_size ** (-0.5)
        v_scr[pl.ds(key_at, TILE), :] = kv_ref[0, :, feat_width:]

    @pl.when(jnp.logical_not(live))
    def _():
        v_scr[pl.ds(key_at, TILE), :] = jnp.zeros((TILE, feat_width), v_scr.dtype)

    @pl.when(slot_at == slot_count - 1)
    def _():
        key_slot = lax.broadcasted_iota(jnp.int32, (TILE, slot_count * TILE), 1) // TILE
        key_live = (key_slot >= KT) | (key_slot < live_count)
        for head in range(HEADS):
            cols = slice(head * head_size, (head + 1) * head_size)
            scores = jnp.where(key_live, s_scr[head], -jnp.inf)
            row_max = jnp.max(scores, axis=-1, keepdims=True)
            weights_raw = jnp.exp(scores - row_max)
            probs = (weights_raw / jnp.sum(weights_raw, axis=-1, keepdims=True)).astype(jnp.bfloat16)
            mixed = jnp.dot(probs, v_scr[:, cols], preferred_element_type=jnp.float32)
            o_ref[0, :, cols] = mixed.astype(o_ref.dtype)


def attend(query_tiles, window, slots, counts):
    tile_count, _, feat_width = query_tiles.shape
    slot_count = KT + GLOBAL

    def kv_map(i, j, slots_ref, counts_ref):
        live_count = counts_ref[i]
        fetch = jnp.where((j >= KT) | (j < live_count), j, jnp.maximum(live_count - 1, 0))
        return (slots_ref[i, fetch], 0, 0)

    grid_spec = pltpu.PrefetchScalarGridSpec(
        num_scalar_prefetch=2,
        grid=(tile_count, slot_count),
        in_specs=[
            pl.BlockSpec((1, TILE, feat_width), lambda i, j, s, c: (i, 0, 0)),
            pl.BlockSpec((1, TILE, 2 * feat_width), kv_map),
        ],
        out_specs=pl.BlockSpec((1, TILE, feat_width), lambda i, j, s, c: (i, 0, 0)),
        scratch_shapes=[
            pltpu.VMEM((HEADS, TILE, slot_count * TILE), jnp.float32),
            pltpu.VMEM((slot_count * TILE, feat_width), jnp.bfloat16),
        ],
    )
    return pl.pallas_call(
        attention_kernel,
        grid_spec=grid_spec,
        out_shape=jax.ShapeDtypeStruct(query_tiles.shape, jnp.bfloat16),
        compiler_params=pltpu.CompilerParams(
            dimension_semantics=("arbitrary", "arbitrary"),
        ),
    )(slots, counts, query_tiles, window)


def local(
    patches,
    vis_index,
    kv_list,
    kv_count,
    global_tiles,
    frame_table,
    space_table,
    ln_gain,
    ln_bias,
    w_qkv,
    w_out,
):
    tok_rows = patches.shape[0]
    feat_width = patches.shape[1]
    tile_count = tok_rows // TILE
    fsdp_size = lax.axis_size("fsdp")
    seq_size = lax.axis_size("seq")
    seq_at = lax.axis_index("seq")
    dev_at = seq_at * fsdp_size + lax.axis_index("fsdp")
    group_tiles = tile_count * fsdp_size

    stream = embed(patches, vis_index, frame_table, space_table)

    dev_count = seq_size * fsdp_size
    global_rows = []
    owners = []
    for slot_no in range(GLOBAL):
        tile_id = global_tiles[slot_no]
        owners.append(tile_id // tile_count)
        global_rows.append(
            lax.dynamic_slice_in_dim(stream, tile_id % tile_count * TILE, TILE, 0)
        )
    global_stream = jnp.stack(global_rows)
    owners = jnp.stack(owners)
    bit_order = sorted(range(dev_count.bit_length() - 1), key=lambda b: -b)
    done_bits = 0
    for bit in bit_order:
        step = 1 << bit
        held = ((dev_at ^ owners) & ~done_bits) == 0
        got = lax.ppermute(
            global_stream, ("seq", "fsdp"), [(i, i ^ step) for i in range(dev_count)]
        )
        global_stream = jnp.where(held[:, None, None], global_stream, got)
        done_bits |= step
    global_stream = global_stream.reshape(GLOBAL * TILE, feat_width)

    w_full = lax.all_gather(w_qkv, "fsdp", axis=0, tiled=True)
    normed = layer_norm(stream, ln_gain, ln_bias)
    qkv = jnp.dot(normed, w_full, preferred_element_type=jnp.float32).astype(jnp.bfloat16)
    query = qkv[:, :feat_width]
    keyval = qkv[:, feat_width:]
    global_normed = layer_norm(global_stream, ln_gain, ln_bias)
    global_kv = jnp.dot(
        global_normed, w_full[:, feat_width:], preferred_element_type=jnp.float32
    ).astype(jnp.bfloat16).reshape(GLOBAL, TILE, 2 * feat_width)

    group_block = lax.all_gather(keyval, "fsdp", axis=0, tiled=True).reshape(
        group_tiles, TILE, 2 * feat_width
    )
    near_blocks = []
    near_rank = []
    for reach in REACH:
        picks, rank = near_tiles(kv_list, seq_at + reach, group_tiles)
        asked = passed_along(picks, "seq", reach)
        near_blocks.append(passed_along(group_block[asked], "seq", -reach))
        near_rank.append(rank)
    window = jnp.concatenate([group_block] + near_blocks + [global_kv], axis=0)
    near_rank = jnp.stack(near_rank)

    entry_group = kv_list // group_tiles
    entry_local = kv_list % group_tiles
    reach_of = entry_group - seq_at
    reach_slot = jnp.where(reach_of < 0, reach_of + 2, reach_of + 1)
    reach_slot = jnp.clip(reach_slot, 0, len(REACH) - 1)
    entry_rank = near_rank[reach_slot, entry_local]
    local_lists = jnp.where(
        reach_of == 0, entry_local, group_tiles + NEAR * reach_slot + jnp.clip(entry_rank, 0, NEAR - 1)
    )
    global_slots = group_tiles + NEAR * len(REACH) + jnp.arange(GLOBAL, dtype=jnp.int32)

    query_tiles = query.reshape(tile_count, TILE, feat_width)
    slots = jnp.concatenate(
        [local_lists, jnp.broadcast_to(global_slots, (tile_count, GLOBAL))], axis=1
    ).astype(jnp.int32)
    heads_out = attend(query_tiles, window, slots, kv_count).reshape(tok_rows, feat_width)
    return jnp.dot(
        heads_out,
        lax.all_gather(w_out, "fsdp", axis=0, tiled=True),
        preferred_element_type=jnp.float32,
    ).astype(jnp.bfloat16)


def solution(mesh):
    return jax.shard_map(
        local,
        mesh=mesh,
        in_specs=(
            P(("seq", "fsdp"), None),
            P(("seq", "fsdp")),
            P(("seq", "fsdp"), None),
            P(("seq", "fsdp")),
            P(),
            P(),
            P(),
            P(),
            P(),
            P("fsdp", None),
            P("fsdp", None),
        ),
        out_specs=P(("seq", "fsdp"), None),
        check_vma=False,
    )
```

```python
import jax
import jax.numpy as jnp
from jax import lax
from jax.experimental import pallas as pl
from jax.experimental.pallas import tpu as pltpu
from jax.sharding import PartitionSpec as P

HEADS = 16
TILE = 128
KT = 16
GLOBAL = 2
PATCHES = 512
NEAR = 3
REACH = (-2, -1, 1, 2)


def passed_along(block, axis, distance):
    devices = range(lax.axis_size(axis))
    route = [(i - distance, i) for i in devices if i - distance in devices]
    return lax.ppermute(block, axis, route)


def layer_norm(stream, ln_gain, ln_bias):
    stream32 = stream.astype(jnp.float32)
    mean_val = jnp.mean(stream32, axis=-1, keepdims=True)
    centred = stream32 - mean_val
    variance = jnp.mean(centred * centred, axis=-1, keepdims=True)
    scaled = centred * lax.rsqrt(variance + 1e-06)
    return (scaled * ln_gain.astype(jnp.float32) + ln_bias.astype(jnp.float32)).astype(jnp.bfloat16)


def embed(patches, vis_index, frame_table, space_table):
    frame_ids = vis_index // PATCHES
    patch_ids = vis_index % PATCHES
    return (
        patches.astype(jnp.float32)
        + frame_table[frame_ids].astype(jnp.float32)
        + space_table[patch_ids].astype(jnp.float32)
    ).astype(jnp.bfloat16)


def near_tiles(entries, group, group_tiles):
    cand = group * group_tiles + jnp.arange(group_tiles, dtype=jnp.int32)
    named = jnp.any(entries.reshape(-1, 1) == cand[None, :], axis=0)
    rank = jnp.cumsum(named.astype(jnp.int32)) - 1
    local_ids = jnp.arange(group_tiles, dtype=jnp.int32)
    picks = jnp.stack(
        [jnp.sum(jnp.where(named & (rank == j), local_ids, 0)) for j in range(NEAR)]
    )
    return picks, rank


def attention_kernel(slots_ref, counts_ref, q_ref, kv_ref, o_ref, s_scr, v_scr):
    tile_at = pl.program_id(0)
    slot_at = pl.program_id(1)
    slot_count = KT + GLOBAL
    feat_width = q_ref.shape[-1]
    head_size = feat_width // HEADS
    live_count = counts_ref[tile_at]
    live = (slot_at >= KT) | (slot_at < live_count)
    key_at = pl.multiple_of(slot_at * TILE, TILE)

    @pl.when(live)
    def _():
        for head in range(HEADS):
            cols = slice(head * head_size, (head + 1) * head_size)
            scores = lax.dot_general(
                q_ref[0, :, cols], kv_ref[0, :, cols], (((1,), (1,)), ((), ())),
                preferred_element_type=jnp.float32,
            )
            s_scr[head, :, pl.ds(key_at, TILE)] = scores * head_size ** (-0.5)
        v_scr[pl.ds(key_at, TILE), :] = kv_ref[0, :, feat_width:]

    @pl.when(jnp.logical_not(live))
    def _():
        v_scr[pl.ds(key_at, TILE), :] = jnp.zeros((TILE, feat_width), v_scr.dtype)

    @pl.when(slot_at == slot_count - 1)
    def _():
        key_slot = lax.broadcasted_iota(jnp.int32, (TILE, slot_count * TILE), 1) // TILE
        key_live = (key_slot >= KT) | (key_slot < live_count)
        for head in range(HEADS):
            cols = slice(head * head_size, (head + 1) * head_size)
            scores = jnp.where(key_live, s_scr[head], -jnp.inf)
            row_max = jnp.max(scores, axis=-1, keepdims=True)
            weights_raw = jnp.exp(scores - row_max)
            probs = (weights_raw / jnp.sum(weights_raw, axis=-1, keepdims=True)).astype(jnp.bfloat16)
            mixed = jnp.dot(probs, v_scr[:, cols], preferred_element_type=jnp.float32)
            o_ref[0, :, cols] = mixed.astype(o_ref.dtype)


def attend(query_tiles, window, slots, counts):
    tile_count, _, feat_width = query_tiles.shape
    slot_count = KT + GLOBAL

    def kv_map(i, j, slots_ref, counts_ref):
        live_count = counts_ref[i]
        fetch = jnp.where((j >= KT) | (j < live_count), j, jnp.maximum(live_count - 1, 0))
        return (slots_ref[i, fetch], 0, 0)

    grid_spec = pltpu.PrefetchScalarGridSpec(
        num_scalar_prefetch=2,
        grid=(tile_count, slot_count),
        in_specs=[
            pl.BlockSpec((1, TILE, feat_width), lambda i, j, s, c: (i, 0, 0)),
            pl.BlockSpec((1, TILE, 2 * feat_width), kv_map),
        ],
        out_specs=pl.BlockSpec((1, TILE, feat_width), lambda i, j, s, c: (i, 0, 0)),
        scratch_shapes=[
            pltpu.VMEM((HEADS, TILE, slot_count * TILE), jnp.float32),
            pltpu.VMEM((slot_count * TILE, feat_width), jnp.bfloat16),
        ],
    )
    return pl.pallas_call(
        attention_kernel,
        grid_spec=grid_spec,
        out_shape=jax.ShapeDtypeStruct(query_tiles.shape, jnp.bfloat16),
        compiler_params=pltpu.CompilerParams(
            dimension_semantics=("arbitrary", "arbitrary"),
        ),
    )(slots, counts, query_tiles, window)


def local(
    patches,
    vis_index,
    kv_list,
    kv_count,
    global_tiles,
    frame_table,
    space_table,
    ln_gain,
    ln_bias,
    w_qkv,
    w_out,
):
    tok_rows = patches.shape[0]
    feat_width = patches.shape[1]
    tile_count = tok_rows // TILE
    fsdp_size = lax.axis_size("fsdp")
    seq_size = lax.axis_size("seq")
    seq_at = lax.axis_index("seq")
    dev_at = seq_at * fsdp_size + lax.axis_index("fsdp")
    group_tiles = tile_count * fsdp_size

    stream = embed(patches, vis_index, frame_table, space_table)

    dev_count = seq_size * fsdp_size
    global_rows = []
    owners = []
    for slot_no in range(GLOBAL):
        tile_id = global_tiles[slot_no]
        owners.append(tile_id // tile_count)
        global_rows.append(
            lax.dynamic_slice_in_dim(stream, tile_id % tile_count * TILE, TILE, 0)
        )
    global_stream = jnp.stack(global_rows)
    owners = jnp.stack(owners)
    bit_order = sorted(range(dev_count.bit_length() - 1), key=lambda b: -b)
    done_bits = 0
    for bit in bit_order:
        step = 1 << bit
        held = ((dev_at ^ owners) & ~done_bits) == 0
        got = lax.ppermute(
            global_stream, ("seq", "fsdp"), [(i, i ^ step) for i in range(dev_count)]
        )
        global_stream = jnp.where(held[:, None, None], global_stream, got)
        done_bits |= step
    global_stream = global_stream.reshape(GLOBAL * TILE, feat_width)

    normed = layer_norm(stream, ln_gain, ln_bias)
    global_normed = layer_norm(global_stream, ln_gain, ln_bias)
    group_rows = lax.all_gather(normed, "fsdp", axis=0, tiled=True).reshape(
        group_tiles, TILE, feat_width
    )
    w_src, group_rows = lax.optimization_barrier((w_qkv, group_rows))
    w_full = lax.all_gather(w_src, "fsdp", axis=0, tiled=True)

    near_blocks = []
    near_rank = []
    for reach in REACH:
        picks, rank = near_tiles(kv_list, seq_at + reach, group_tiles)
        asked = passed_along(picks, "seq", reach)
        near_blocks.append(passed_along(group_rows[asked], "seq", -reach))
        near_rank.append(rank)
    window_rows = jnp.concatenate(
        [group_rows] + near_blocks + [global_normed.reshape(GLOBAL, TILE, feat_width)], axis=0
    )
    window = jnp.dot(
        window_rows.reshape(-1, feat_width), w_full[:, feat_width:],
        preferred_element_type=jnp.float32,
    ).astype(jnp.bfloat16).reshape(-1, TILE, 2 * feat_width)
    query = jnp.dot(
        normed, w_full[:, :feat_width], preferred_element_type=jnp.float32
    ).astype(jnp.bfloat16)
    near_rank = jnp.stack(near_rank)

    entry_group = kv_list // group_tiles
    entry_local = kv_list % group_tiles
    reach_of = entry_group - seq_at
    reach_slot = jnp.where(reach_of < 0, reach_of + 2, reach_of + 1)
    reach_slot = jnp.clip(reach_slot, 0, len(REACH) - 1)
    entry_rank = near_rank[reach_slot, entry_local]
    local_lists = jnp.where(
        reach_of == 0, entry_local, group_tiles + NEAR * reach_slot + jnp.clip(entry_rank, 0, NEAR - 1)
    )
    global_slots = group_tiles + NEAR * len(REACH) + jnp.arange(GLOBAL, dtype=jnp.int32)

    query_tiles = query.reshape(tile_count, TILE, feat_width)
    slots = jnp.concatenate(
        [local_lists, jnp.broadcast_to(global_slots, (tile_count, GLOBAL))], axis=1
    ).astype(jnp.int32)
    heads_out = attend(query_tiles, window, slots, kv_count).reshape(tok_rows, feat_width)
    return jnp.dot(
        heads_out,
        lax.all_gather(w_out, "fsdp", axis=0, tiled=True),
        preferred_element_type=jnp.float32,
    ).astype(jnp.bfloat16)


def solution(mesh):
    return jax.shard_map(
        local,
        mesh=mesh,
        in_specs=(
            P(("seq", "fsdp"), None),
            P(("seq", "fsdp")),
            P(("seq", "fsdp"), None),
            P(("seq", "fsdp")),
            P(),
            P(),
            P(),
            P(),
            P(),
            P("fsdp", None),
            P("fsdp", None),
        ),
        out_specs=P(("seq", "fsdp"), None),
        check_vma=False,
    )
```

```python
import jax
import jax.numpy as jnp
from jax import lax
from jax.experimental import pallas as pl
from jax.experimental.pallas import tpu as pltpu
from jax.sharding import PartitionSpec as P

HEADS = 16
TILE = 128
KT = 16
GLOBAL = 2
PATCHES = 512
NEAR = 3
REACH = (-2, -1, 1, 2)


def passed_along(block, axis, distance):
    devices = range(lax.axis_size(axis))
    route = [(i - distance, i) for i in devices if i - distance in devices]
    return lax.ppermute(block, axis, route)


def gathered_weight(shard):
    core = lax.axis_index("seq") % 2
    half = shard.shape[1] // 2
    mine = lax.all_gather(
        lax.dynamic_slice_in_dim(shard, core * half, half, 1), "fsdp", axis=0, tiled=True
    )
    seq_size = lax.axis_size("seq")
    other = lax.ppermute(mine, "seq", [(i, i ^ 1) for i in range(seq_size)])
    low = jnp.where(core == 0, mine, other)
    high = jnp.where(core == 0, other, mine)
    return jnp.concatenate([low, high], axis=1)


def layer_norm(stream, ln_gain, ln_bias):
    stream32 = stream.astype(jnp.float32)
    mean_val = jnp.mean(stream32, axis=-1, keepdims=True)
    centred = stream32 - mean_val
    variance = jnp.mean(centred * centred, axis=-1, keepdims=True)
    scaled = centred * lax.rsqrt(variance + 1e-06)
    return (scaled * ln_gain.astype(jnp.float32) + ln_bias.astype(jnp.float32)).astype(jnp.bfloat16)


def embed(patches, vis_index, frame_table, space_table):
    frame_ids = vis_index // PATCHES
    patch_ids = vis_index % PATCHES
    return (
        patches.astype(jnp.float32)
        + frame_table[frame_ids].astype(jnp.float32)
        + space_table[patch_ids].astype(jnp.float32)
    ).astype(jnp.bfloat16)


def near_tiles(entries, group, group_tiles):
    cand = group * group_tiles + jnp.arange(group_tiles, dtype=jnp.int32)
    named = jnp.any(entries.reshape(-1, 1) == cand[None, :], axis=0)
    rank = jnp.cumsum(named.astype(jnp.int32)) - 1
    local_ids = jnp.arange(group_tiles, dtype=jnp.int32)
    picks = jnp.stack(
        [jnp.sum(jnp.where(named & (rank == j), local_ids, 0)) for j in range(NEAR)]
    )
    return picks, rank


def attention_kernel(slots_ref, counts_ref, q_ref, kv_ref, o_ref, s_scr, v_scr):
    tile_at = pl.program_id(0)
    slot_at = pl.program_id(1)
    slot_count = KT + GLOBAL
    feat_width = q_ref.shape[-1]
    head_size = feat_width // HEADS
    live_count = counts_ref[tile_at]
    live = (slot_at >= KT) | (slot_at < live_count)
    key_at = pl.multiple_of(slot_at * TILE, TILE)

    @pl.when(live)
    def _():
        for head in range(HEADS):
            cols = slice(head * head_size, (head + 1) * head_size)
            scores = lax.dot_general(
                q_ref[0, :, cols], kv_ref[0, :, cols], (((1,), (1,)), ((), ())),
                preferred_element_type=jnp.float32,
            )
            s_scr[head, :, pl.ds(key_at, TILE)] = scores * head_size ** (-0.5)
        v_scr[pl.ds(key_at, TILE), :] = kv_ref[0, :, feat_width:]

    @pl.when(jnp.logical_not(live))
    def _():
        v_scr[pl.ds(key_at, TILE), :] = jnp.zeros((TILE, feat_width), v_scr.dtype)

    @pl.when(slot_at == slot_count - 1)
    def _():
        key_slot = lax.broadcasted_iota(jnp.int32, (TILE, slot_count * TILE), 1) // TILE
        key_live = (key_slot >= KT) | (key_slot < live_count)
        for head in range(HEADS):
            cols = slice(head * head_size, (head + 1) * head_size)
            scores = jnp.where(key_live, s_scr[head], -jnp.inf)
            row_max = jnp.max(scores, axis=-1, keepdims=True)
            weights_raw = jnp.exp(scores - row_max)
            probs = (weights_raw / jnp.sum(weights_raw, axis=-1, keepdims=True)).astype(jnp.bfloat16)
            mixed = jnp.dot(probs, v_scr[:, cols], preferred_element_type=jnp.float32)
            o_ref[0, :, cols] = mixed.astype(o_ref.dtype)


def attend(query_tiles, window, slots, counts):
    tile_count, _, feat_width = query_tiles.shape
    slot_count = KT + GLOBAL

    def kv_map(i, j, slots_ref, counts_ref):
        live_count = counts_ref[i]
        fetch = jnp.where((j >= KT) | (j < live_count), j, jnp.maximum(live_count - 1, 0))
        return (slots_ref[i, fetch], 0, 0)

    grid_spec = pltpu.PrefetchScalarGridSpec(
        num_scalar_prefetch=2,
        grid=(tile_count, slot_count),
        in_specs=[
            pl.BlockSpec((1, TILE, feat_width), lambda i, j, s, c: (i, 0, 0)),
            pl.BlockSpec((1, TILE, 2 * feat_width), kv_map),
        ],
        out_specs=pl.BlockSpec((1, TILE, feat_width), lambda i, j, s, c: (i, 0, 0)),
        scratch_shapes=[
            pltpu.VMEM((HEADS, TILE, slot_count * TILE), jnp.float32),
            pltpu.VMEM((slot_count * TILE, feat_width), jnp.bfloat16),
        ],
    )
    return pl.pallas_call(
        attention_kernel,
        grid_spec=grid_spec,
        out_shape=jax.ShapeDtypeStruct(query_tiles.shape, jnp.bfloat16),
        compiler_params=pltpu.CompilerParams(
            dimension_semantics=("arbitrary", "arbitrary"),
        ),
    )(slots, counts, query_tiles, window)


def local(
    patches,
    vis_index,
    kv_list,
    kv_count,
    global_tiles,
    frame_table,
    space_table,
    ln_gain,
    ln_bias,
    w_qkv,
    w_out,
):
    tok_rows = patches.shape[0]
    feat_width = patches.shape[1]
    tile_count = tok_rows // TILE
    fsdp_size = lax.axis_size("fsdp")
    seq_size = lax.axis_size("seq")
    seq_at = lax.axis_index("seq")
    group_tiles = tile_count * fsdp_size

    stream = embed(patches, vis_index, frame_table, space_table)

    normed = layer_norm(stream, ln_gain, ln_bias)
    group_rows = lax.all_gather(normed, "fsdp", axis=0, tiled=True).reshape(
        group_tiles, TILE, feat_width
    )
    w_src, group_rows = lax.optimization_barrier((w_qkv, group_rows))
    w_full = gathered_weight(w_src)

    global_ids = global_tiles.astype(jnp.int32)
    global_rows = group_rows[global_ids % group_tiles]
    owners = global_ids // group_tiles
    for bit in sorted(range(seq_size.bit_length() - 1), key=lambda b: -b):
        step = 1 << bit
        held = ((seq_at ^ owners) & (2 * step - 1)) == 0
        got = lax.ppermute(global_rows, "seq", [(i, i ^ step) for i in range(seq_size)])
        global_rows = jnp.where(held[:, None, None], global_rows, got)
    near_blocks = []
    near_rank = []
    for reach in REACH:
        picks, rank = near_tiles(kv_list, seq_at + reach, group_tiles)
        asked = passed_along(picks, "seq", reach)
        near_blocks.append(passed_along(group_rows[asked], "seq", -reach))
        near_rank.append(rank)
    window_rows = jnp.concatenate(
        [group_rows] + near_blocks + [global_rows], axis=0
    )
    window = jnp.dot(
        window_rows.reshape(-1, feat_width), w_full[:, feat_width:],
        preferred_element_type=jnp.float32,
    ).astype(jnp.bfloat16).reshape(-1, TILE, 2 * feat_width)
    query = jnp.dot(
        normed, w_full[:, :feat_width], preferred_element_type=jnp.float32
    ).astype(jnp.bfloat16)
    near_rank = jnp.stack(near_rank)

    entry_group = kv_list // group_tiles
    entry_local = kv_list % group_tiles
    reach_of = entry_group - seq_at
    reach_slot = jnp.where(reach_of < 0, reach_of + 2, reach_of + 1)
    reach_slot = jnp.clip(reach_slot, 0, len(REACH) - 1)
    entry_rank = near_rank[reach_slot, entry_local]
    local_lists = jnp.where(
        reach_of == 0, entry_local, group_tiles + NEAR * reach_slot + jnp.clip(entry_rank, 0, NEAR - 1)
    )
    global_slots = group_tiles + NEAR * len(REACH) + jnp.arange(GLOBAL, dtype=jnp.int32)

    query_tiles = query.reshape(tile_count, TILE, feat_width)
    slots = jnp.concatenate(
        [local_lists, jnp.broadcast_to(global_slots, (tile_count, GLOBAL))], axis=1
    ).astype(jnp.int32)
    heads_out = attend(query_tiles, window, slots, kv_count).reshape(tok_rows, feat_width)
    return jnp.dot(
        heads_out,
        gathered_weight(w_out),
        preferred_element_type=jnp.float32,
    ).astype(jnp.bfloat16)


def solution(mesh):
    return jax.shard_map(
        local,
        mesh=mesh,
        in_specs=(
            P(("seq", "fsdp"), None),
            P(("seq", "fsdp")),
            P(("seq", "fsdp"), None),
            P(("seq", "fsdp")),
            P(),
            P(),
            P(),
            P(),
            P(),
            P("fsdp", None),
            P("fsdp", None),
        ),
        out_specs=P(("seq", "fsdp"), None),
        check_vma=False,
    )
```

```python
import jax
import jax.numpy as jnp
from jax import lax
from jax.experimental import pallas as pl
from jax.experimental.pallas import tpu as pltpu
from jax.sharding import PartitionSpec as P

HEADS = 16
TILE = 128
KT = 16
GLOBAL = 2
PATCHES = 512
NEAR = 3
REACH = (-2, -1, 1, 2)


def passed_along(block, axis, distance):
    devices = range(lax.axis_size(axis))
    route = [(i - distance, i) for i in devices if i - distance in devices]
    return lax.ppermute(block, axis, route)


def gathered_weight(shard):
    core = lax.axis_index("seq") % 2
    half = shard.shape[1] // 2
    mine = lax.all_gather(
        lax.dynamic_slice_in_dim(shard, core * half, half, 1), "fsdp", axis=0, tiled=True
    )
    seq_size = lax.axis_size("seq")
    other = lax.ppermute(mine, "seq", [(i, i ^ 1) for i in range(seq_size)])
    low = jnp.where(core == 0, mine, other)
    high = jnp.where(core == 0, other, mine)
    return jnp.concatenate([low, high], axis=1)


def layer_norm(stream, ln_gain, ln_bias):
    stream32 = stream.astype(jnp.float32)
    mean_val = jnp.mean(stream32, axis=-1, keepdims=True)
    centred = stream32 - mean_val
    variance = jnp.mean(centred * centred, axis=-1, keepdims=True)
    scaled = centred * lax.rsqrt(variance + 1e-06)
    return (scaled * ln_gain.astype(jnp.float32) + ln_bias.astype(jnp.float32)).astype(jnp.bfloat16)


def embed(patches, vis_index, frame_table, space_table):
    frame_ids = vis_index // PATCHES
    patch_ids = vis_index % PATCHES
    return (
        patches.astype(jnp.float32)
        + frame_table[frame_ids].astype(jnp.float32)
        + space_table[patch_ids].astype(jnp.float32)
    ).astype(jnp.bfloat16)


def near_tiles(entries, group, group_tiles):
    cand = group * group_tiles + jnp.arange(group_tiles, dtype=jnp.int32)
    named = jnp.any(entries.reshape(-1, 1) == cand[None, :], axis=0)
    rank = jnp.cumsum(named.astype(jnp.int32)) - 1
    local_ids = jnp.arange(group_tiles, dtype=jnp.int32)
    picks = jnp.stack(
        [jnp.sum(jnp.where(named & (rank == j), local_ids, 0)) for j in range(NEAR)]
    )
    return picks, rank


def attention_kernel(slots_ref, counts_ref, q_ref, kv_ref, o_ref, s_scr, v_scr):
    tile_at = pl.program_id(0)
    slot_at = pl.program_id(1)
    slot_count = KT + GLOBAL
    feat_width = q_ref.shape[-1]
    head_size = feat_width // HEADS
    live_count = counts_ref[tile_at]
    live = (slot_at >= KT) | (slot_at < live_count)
    key_at = pl.multiple_of(slot_at * TILE, TILE)

    @pl.when(live)
    def _():
        for head in range(HEADS):
            cols = slice(head * head_size, (head + 1) * head_size)
            scores = lax.dot_general(
                q_ref[0, :, cols], kv_ref[0, :, cols], (((1,), (1,)), ((), ())),
                preferred_element_type=jnp.float32,
            )
            s_scr[head, :, pl.ds(key_at, TILE)] = scores * head_size ** (-0.5)
        v_scr[pl.ds(key_at, TILE), :] = kv_ref[0, :, feat_width:]

    @pl.when(jnp.logical_not(live))
    def _():
        v_scr[pl.ds(key_at, TILE), :] = jnp.zeros((TILE, feat_width), v_scr.dtype)

    @pl.when(slot_at == slot_count - 1)
    def _():
        key_slot = lax.broadcasted_iota(jnp.int32, (TILE, slot_count * TILE), 1) // TILE
        key_live = (key_slot >= KT) | (key_slot < live_count)
        for head in range(HEADS):
            cols = slice(head * head_size, (head + 1) * head_size)
            scores = jnp.where(key_live, s_scr[head], -jnp.inf)
            row_max = jnp.max(scores, axis=-1, keepdims=True)
            weights_raw = jnp.exp(scores - row_max)
            probs = (weights_raw / jnp.sum(weights_raw, axis=-1, keepdims=True)).astype(jnp.bfloat16)
            mixed = jnp.dot(probs, v_scr[:, cols], preferred_element_type=jnp.float32)
            o_ref[0, :, cols] = mixed.astype(o_ref.dtype)


def attend(query_tiles, window, slots, counts):
    tile_count, _, feat_width = query_tiles.shape
    slot_count = KT + GLOBAL

    def kv_map(i, j, slots_ref, counts_ref):
        live_count = counts_ref[i]
        fetch = jnp.where((j >= KT) | (j < live_count), j, jnp.maximum(live_count - 1, 0))
        return (slots_ref[i, fetch], 0, 0)

    grid_spec = pltpu.PrefetchScalarGridSpec(
        num_scalar_prefetch=2,
        grid=(tile_count, slot_count),
        in_specs=[
            pl.BlockSpec((1, TILE, feat_width), lambda i, j, s, c: (i, 0, 0)),
            pl.BlockSpec((1, TILE, 2 * feat_width), kv_map),
        ],
        out_specs=pl.BlockSpec((1, TILE, feat_width), lambda i, j, s, c: (i, 0, 0)),
        scratch_shapes=[
            pltpu.VMEM((HEADS, TILE, slot_count * TILE), jnp.float32),
            pltpu.VMEM((slot_count * TILE, feat_width), jnp.bfloat16),
        ],
    )
    return pl.pallas_call(
        attention_kernel,
        grid_spec=grid_spec,
        out_shape=jax.ShapeDtypeStruct(query_tiles.shape, jnp.bfloat16),
        compiler_params=pltpu.CompilerParams(
            dimension_semantics=("arbitrary", "arbitrary"),
        ),
    )(slots, counts, query_tiles, window)


def local(
    patches,
    vis_index,
    kv_list,
    kv_count,
    global_tiles,
    frame_table,
    space_table,
    ln_gain,
    ln_bias,
    w_qkv,
    w_out,
):
    tok_rows = patches.shape[0]
    feat_width = patches.shape[1]
    tile_count = tok_rows // TILE
    fsdp_size = lax.axis_size("fsdp")
    seq_size = lax.axis_size("seq")
    seq_at = lax.axis_index("seq")
    group_tiles = tile_count * fsdp_size

    stream = embed(patches, vis_index, frame_table, space_table)

    normed = layer_norm(stream, ln_gain, ln_bias)
    group_rows = lax.all_gather(normed, "fsdp", axis=0, tiled=True).reshape(
        group_tiles, TILE, feat_width
    )

    def tiles_at(ids):
        return jnp.concatenate(
            [lax.dynamic_slice_in_dim(group_rows, ids[n], 1, 0) for n in range(ids.shape[0])]
        )

    global_ids = global_tiles.astype(jnp.int32)
    global_rows = tiles_at(global_ids % group_tiles)
    owners = global_ids // group_tiles

    sends = []
    near_rank = []
    for reach in REACH:
        picks, rank = near_tiles(kv_list, seq_at + reach, group_tiles)
        sends.append(tiles_at(passed_along(picks, "seq", reach)))
        near_rank.append(rank)

    w_src, global_rows, sends = lax.optimization_barrier((w_qkv, global_rows, sends))
    w_full = gathered_weight(w_src)
    near_blocks = [passed_along(sent, "seq", -reach) for sent, reach in zip(sends, REACH)]
    for bit in sorted(range(seq_size.bit_length() - 1), key=lambda b: -b):
        step = 1 << bit
        held = ((seq_at ^ owners) & (2 * step - 1)) == 0
        got = lax.ppermute(global_rows, "seq", [(i, i ^ step) for i in range(seq_size)])
        global_rows = jnp.where(held[:, None, None], global_rows, got)
    window_rows = jnp.concatenate(
        [group_rows] + near_blocks + [global_rows], axis=0
    )
    w_out_src, window_rows = lax.optimization_barrier((w_out, window_rows))
    window = jnp.dot(
        window_rows.reshape(-1, feat_width), w_full[:, feat_width:],
        preferred_element_type=jnp.float32,
    ).astype(jnp.bfloat16).reshape(-1, TILE, 2 * feat_width)
    query = jnp.dot(
        normed, w_full[:, :feat_width], preferred_element_type=jnp.float32
    ).astype(jnp.bfloat16)
    near_rank = jnp.stack(near_rank)

    entry_group = kv_list // group_tiles
    entry_local = kv_list % group_tiles
    reach_of = entry_group - seq_at
    reach_slot = jnp.where(reach_of < 0, reach_of + 2, reach_of + 1)
    reach_slot = jnp.clip(reach_slot, 0, len(REACH) - 1)
    entry_rank = near_rank[reach_slot, entry_local]
    local_lists = jnp.where(
        reach_of == 0, entry_local, group_tiles + NEAR * reach_slot + jnp.clip(entry_rank, 0, NEAR - 1)
    )
    global_slots = group_tiles + NEAR * len(REACH) + jnp.arange(GLOBAL, dtype=jnp.int32)

    query_tiles = query.reshape(tile_count, TILE, feat_width)
    slots = jnp.concatenate(
        [local_lists, jnp.broadcast_to(global_slots, (tile_count, GLOBAL))], axis=1
    ).astype(jnp.int32)
    heads_out = attend(query_tiles, window, slots, kv_count).reshape(tok_rows, feat_width)
    return jnp.dot(
        heads_out,
        gathered_weight(w_out_src),
        preferred_element_type=jnp.float32,
    ).astype(jnp.bfloat16)


def solution(mesh):
    return jax.shard_map(
        local,
        mesh=mesh,
        in_specs=(
            P(("seq", "fsdp"), None),
            P(("seq", "fsdp")),
            P(("seq", "fsdp"), None),
            P(("seq", "fsdp")),
            P(),
            P(),
            P(),
            P(),
            P(),
            P("fsdp", None),
            P("fsdp", None),
        ),
        out_specs=P(("seq", "fsdp"), None),
        check_vma=False,
    )
```

```python
import jax
import jax.numpy as jnp
from jax import lax
from jax.experimental import pallas as pl
from jax.experimental.pallas import tpu as pltpu
from jax.sharding import PartitionSpec as P

HEADS = 16
TILE = 128
KT = 16
GLOBAL = 2
PATCHES = 512
NEAR = 3
REACH = (-2, -1, 1, 2)


def passed_along(block, axis, distance):
    devices = range(lax.axis_size(axis))
    route = [(i - distance, i) for i in devices if i - distance in devices]
    return lax.ppermute(block, axis, route)


def gathered_weight(shard):
    core = lax.axis_index("seq") % 2
    half = shard.shape[1] // 2
    mine = lax.all_gather(
        lax.dynamic_slice_in_dim(shard, core * half, half, 1), "fsdp", axis=0, tiled=True
    )
    seq_size = lax.axis_size("seq")
    other = lax.ppermute(mine, "seq", [(i, i ^ 1) for i in range(seq_size)])
    low = jnp.where(core == 0, mine, other)
    high = jnp.where(core == 0, other, mine)
    return jnp.concatenate([low, high], axis=1)


def layer_norm(stream, ln_gain, ln_bias):
    stream32 = stream.astype(jnp.float32)
    mean_val = jnp.mean(stream32, axis=-1, keepdims=True)
    centred = stream32 - mean_val
    variance = jnp.mean(centred * centred, axis=-1, keepdims=True)
    scaled = centred * lax.rsqrt(variance + 1e-06)
    return (scaled * ln_gain.astype(jnp.float32) + ln_bias.astype(jnp.float32)).astype(jnp.bfloat16)


def embed(patches, vis_index, frame_table, space_table):
    frame_ids = vis_index // PATCHES
    patch_ids = vis_index % PATCHES
    return (
        patches.astype(jnp.float32)
        + frame_table[frame_ids].astype(jnp.float32)
        + space_table[patch_ids].astype(jnp.float32)
    ).astype(jnp.bfloat16)


def near_tiles(entries, group, group_tiles):
    cand = group * group_tiles + jnp.arange(group_tiles, dtype=jnp.int32)
    named = jnp.any(entries.reshape(-1, 1) == cand[None, :], axis=0)
    rank = jnp.cumsum(named.astype(jnp.int32)) - 1
    local_ids = jnp.arange(group_tiles, dtype=jnp.int32)
    picks = jnp.stack(
        [jnp.sum(jnp.where(named & (rank == j), local_ids, 0)) for j in range(NEAR)]
    )
    return picks, rank


def attention_kernel(slots_ref, counts_ref, q_ref, kv_ref, o_ref, s_scr, v_scr):
    tile_at = pl.program_id(0)
    slot_at = pl.program_id(1)
    slot_count = KT + GLOBAL
    feat_width = q_ref.shape[-1]
    head_size = feat_width // HEADS
    live_count = counts_ref[tile_at]
    live = (slot_at >= KT) | (slot_at < live_count)
    key_at = pl.multiple_of(slot_at * TILE, TILE)

    @pl.when(live)
    def _():
        for head in range(HEADS):
            cols = slice(head * head_size, (head + 1) * head_size)
            scores = lax.dot_general(
                q_ref[0, :, cols], kv_ref[0, :, cols], (((1,), (1,)), ((), ())),
                preferred_element_type=jnp.float32,
            )
            s_scr[head, :, pl.ds(key_at, TILE)] = scores * head_size ** (-0.5)
        v_scr[pl.ds(key_at, TILE), :] = kv_ref[0, :, feat_width:]

    @pl.when(jnp.logical_not(live))
    def _():
        v_scr[pl.ds(key_at, TILE), :] = jnp.zeros((TILE, feat_width), v_scr.dtype)

    @pl.when(slot_at == slot_count - 1)
    def _():
        key_slot = lax.broadcasted_iota(jnp.int32, (TILE, slot_count * TILE), 1) // TILE
        key_live = (key_slot >= KT) | (key_slot < live_count)
        for head in range(HEADS):
            cols = slice(head * head_size, (head + 1) * head_size)
            scores = jnp.where(key_live, s_scr[head], -jnp.inf)
            row_max = jnp.max(scores, axis=-1, keepdims=True)
            weights_raw = jnp.exp(scores - row_max)
            probs = (weights_raw / jnp.sum(weights_raw, axis=-1, keepdims=True)).astype(jnp.bfloat16)
            mixed = jnp.dot(probs, v_scr[:, cols], preferred_element_type=jnp.float32)
            o_ref[0, :, cols] = mixed.astype(o_ref.dtype)


def attend(query_tiles, window, slots, counts):
    tile_count, _, feat_width = query_tiles.shape
    slot_count = KT + GLOBAL

    def kv_map(i, j, slots_ref, counts_ref):
        live_count = counts_ref[i]
        fetch = jnp.where((j >= KT) | (j < live_count), j, jnp.maximum(live_count - 1, 0))
        return (slots_ref[i, fetch], 0, 0)

    grid_spec = pltpu.PrefetchScalarGridSpec(
        num_scalar_prefetch=2,
        grid=(tile_count, slot_count),
        in_specs=[
            pl.BlockSpec((1, TILE, feat_width), lambda i, j, s, c: (i, 0, 0)),
            pl.BlockSpec((1, TILE, 2 * feat_width), kv_map),
        ],
        out_specs=pl.BlockSpec((1, TILE, feat_width), lambda i, j, s, c: (i, 0, 0)),
        scratch_shapes=[
            pltpu.VMEM((HEADS, TILE, slot_count * TILE), jnp.float32),
            pltpu.VMEM((slot_count * TILE, feat_width), jnp.bfloat16),
        ],
    )
    return pl.pallas_call(
        attention_kernel,
        grid_spec=grid_spec,
        out_shape=jax.ShapeDtypeStruct(query_tiles.shape, jnp.bfloat16),
        compiler_params=pltpu.CompilerParams(
            dimension_semantics=("arbitrary", "arbitrary"),
        ),
    )(slots, counts, query_tiles, window)


def local(
    patches,
    vis_index,
    kv_list,
    kv_count,
    global_tiles,
    frame_table,
    space_table,
    ln_gain,
    ln_bias,
    w_qkv,
    w_out,
):
    tok_rows = patches.shape[0]
    feat_width = patches.shape[1]
    tile_count = tok_rows // TILE
    fsdp_size = lax.axis_size("fsdp")
    seq_size = lax.axis_size("seq")
    seq_at = lax.axis_index("seq")
    group_tiles = tile_count * fsdp_size

    stream = embed(patches, vis_index, frame_table, space_table)

    normed = layer_norm(stream, ln_gain, ln_bias)
    group_rows = lax.all_gather(normed, "fsdp", axis=0, tiled=True).reshape(
        group_tiles, TILE, feat_width
    )

    def tiles_at(ids):
        return jnp.concatenate(
            [lax.dynamic_slice_in_dim(group_rows, ids[n], 1, 0) for n in range(ids.shape[0])]
        )

    global_ids = global_tiles.astype(jnp.int32)
    global_rows = tiles_at(global_ids % group_tiles)
    owners = global_ids // group_tiles

    sends = []
    near_rank = []
    for reach in REACH:
        picks, rank = near_tiles(kv_list, seq_at + reach, group_tiles)
        sends.append(tiles_at(passed_along(picks, "seq", reach)))
        near_rank.append(rank)

    w_src, global_rows, sends = lax.optimization_barrier((w_qkv, global_rows, sends))
    w_full = gathered_weight(w_src)
    near_blocks = [passed_along(sent, "seq", -reach) for sent, reach in zip(sends, REACH)]
    seq_bits = seq_size.bit_length() - 1
    digits = [(max(top - 2, 0), top - max(top - 2, 0)) for top in range(seq_bits, 0, -2)]
    for low, width in digits:
        diff = ((seq_at ^ owners) >> low) & ((1 << width) - 1)
        mixed = global_rows
        for k in range(1, 1 << width):
            got = lax.ppermute(
                global_rows, "seq", [(i, i ^ (k << low)) for i in range(seq_size)]
            )
            mixed = jnp.where((diff == k)[:, None, None], got, mixed)
        global_rows = mixed
    window_rows = jnp.concatenate(
        [group_rows] + near_blocks + [global_rows], axis=0
    )
    window = jnp.dot(
        window_rows.reshape(-1, feat_width), w_full[:, feat_width:],
        preferred_element_type=jnp.float32,
    ).astype(jnp.bfloat16).reshape(-1, TILE, 2 * feat_width)
    query = jnp.dot(
        normed, w_full[:, :feat_width], preferred_element_type=jnp.float32
    ).astype(jnp.bfloat16)
    near_rank = jnp.stack(near_rank)

    entry_group = kv_list // group_tiles
    entry_local = kv_list % group_tiles
    reach_of = entry_group - seq_at
    reach_slot = jnp.where(reach_of < 0, reach_of + 2, reach_of + 1)
    reach_slot = jnp.clip(reach_slot, 0, len(REACH) - 1)
    entry_rank = near_rank[reach_slot, entry_local]
    local_lists = jnp.where(
        reach_of == 0, entry_local, group_tiles + NEAR * reach_slot + jnp.clip(entry_rank, 0, NEAR - 1)
    )
    global_slots = group_tiles + NEAR * len(REACH) + jnp.arange(GLOBAL, dtype=jnp.int32)

    query_tiles = query.reshape(tile_count, TILE, feat_width)
    slots = jnp.concatenate(
        [local_lists, jnp.broadcast_to(global_slots, (tile_count, GLOBAL))], axis=1
    ).astype(jnp.int32)
    heads_out = attend(query_tiles, window, slots, kv_count).reshape(tok_rows, feat_width)
    return jnp.dot(
        heads_out,
        lax.all_gather(w_out, "fsdp", axis=0, tiled=True),
        preferred_element_type=jnp.float32,
    ).astype(jnp.bfloat16)


def solution(mesh):
    return jax.shard_map(
        local,
        mesh=mesh,
        in_specs=(
            P(("seq", "fsdp"), None),
            P(("seq", "fsdp")),
            P(("seq", "fsdp"), None),
            P(("seq", "fsdp")),
            P(),
            P(),
            P(),
            P(),
            P(),
            P("fsdp", None),
            P("fsdp", None),
        ),
        out_specs=P(("seq", "fsdp"), None),
        check_vma=False,
    )
```

```python
import jax
import jax.numpy as jnp
from jax import lax
from jax.experimental import pallas as pl
from jax.experimental.pallas import tpu as pltpu
from jax.sharding import PartitionSpec as P

HEADS = 16
TILE = 128
KT = 16
GLOBAL = 2
PATCHES = 512
NEAR = 3
REACH = (-2, -1, 1, 2)


def passed_along(block, axis, distance):
    devices = range(lax.axis_size(axis))
    route = [(i - distance, i) for i in devices if i - distance in devices]
    return lax.ppermute(block, axis, route)


def gathered_weight(shard):
    core = lax.axis_index("seq") % 2
    half = shard.shape[1] // 2
    mine = lax.all_gather(
        lax.dynamic_slice_in_dim(shard, core * half, half, 1), "fsdp", axis=0, tiled=True
    )
    seq_size = lax.axis_size("seq")
    other = lax.ppermute(mine, "seq", [(i, i ^ 1) for i in range(seq_size)])
    low = jnp.where(core == 0, mine, other)
    high = jnp.where(core == 0, other, mine)
    return jnp.concatenate([low, high], axis=1)


def layer_norm(stream, ln_gain, ln_bias):
    stream32 = stream.astype(jnp.float32)
    mean_val = jnp.mean(stream32, axis=-1, keepdims=True)
    centred = stream32 - mean_val
    variance = jnp.mean(centred * centred, axis=-1, keepdims=True)
    scaled = centred * lax.rsqrt(variance + 1e-06)
    return (scaled * ln_gain.astype(jnp.float32) + ln_bias.astype(jnp.float32)).astype(jnp.bfloat16)


def embed(patches, vis_index, frame_table, space_table):
    frame_ids = vis_index // PATCHES
    patch_ids = vis_index % PATCHES
    return (
        patches.astype(jnp.float32)
        + frame_table[frame_ids].astype(jnp.float32)
        + space_table[patch_ids].astype(jnp.float32)
    ).astype(jnp.bfloat16)


def near_tiles(entries, group, group_tiles):
    cand = group * group_tiles + jnp.arange(group_tiles, dtype=jnp.int32)
    named = jnp.any(entries.reshape(-1, 1) == cand[None, :], axis=0)
    rank = jnp.cumsum(named.astype(jnp.int32)) - 1
    local_ids = jnp.arange(group_tiles, dtype=jnp.int32)
    picks = jnp.stack(
        [jnp.sum(jnp.where(named & (rank == j), local_ids, 0)) for j in range(NEAR)]
    )
    return picks, rank


def attention_kernel(slots_ref, counts_ref, q_ref, kv_ref, o_ref, s_scr, v_scr):
    tile_at = pl.program_id(0)
    slot_at = pl.program_id(1)
    slot_count = KT + GLOBAL
    feat_width = q_ref.shape[-1]
    head_size = feat_width // HEADS
    live_count = counts_ref[tile_at]
    live = (slot_at >= KT) | (slot_at < live_count)
    key_at = pl.multiple_of(slot_at * TILE, TILE)

    @pl.when(live)
    def _():
        for head in range(HEADS):
            cols = slice(head * head_size, (head + 1) * head_size)
            scores = lax.dot_general(
                q_ref[0, :, cols], kv_ref[0, :, cols], (((1,), (1,)), ((), ())),
                preferred_element_type=jnp.float32,
            )
            s_scr[head, :, pl.ds(key_at, TILE)] = scores * head_size ** (-0.5)
        v_scr[pl.ds(key_at, TILE), :] = kv_ref[0, :, feat_width:]

    @pl.when(jnp.logical_not(live))
    def _():
        v_scr[pl.ds(key_at, TILE), :] = jnp.zeros((TILE, feat_width), v_scr.dtype)

    @pl.when(slot_at == slot_count - 1)
    def _():
        key_slot = lax.broadcasted_iota(jnp.int32, (TILE, slot_count * TILE), 1) // TILE
        key_live = (key_slot >= KT) | (key_slot < live_count)
        for head in range(HEADS):
            cols = slice(head * head_size, (head + 1) * head_size)
            scores = jnp.where(key_live, s_scr[head], -jnp.inf)
            row_max = jnp.max(scores, axis=-1, keepdims=True)
            weights_raw = jnp.exp(scores - row_max)
            probs = (weights_raw / jnp.sum(weights_raw, axis=-1, keepdims=True)).astype(jnp.bfloat16)
            mixed = jnp.dot(probs, v_scr[:, cols], preferred_element_type=jnp.float32)
            o_ref[0, :, cols] = mixed.astype(o_ref.dtype)


def attend(query_tiles, window, slots, counts):
    tile_count, _, feat_width = query_tiles.shape
    slot_count = KT + GLOBAL

    def kv_map(i, j, slots_ref, counts_ref):
        live_count = counts_ref[i]
        fetch = jnp.where((j >= KT) | (j < live_count), j, jnp.maximum(live_count - 1, 0))
        return (slots_ref[i, fetch], 0, 0)

    grid_spec = pltpu.PrefetchScalarGridSpec(
        num_scalar_prefetch=2,
        grid=(tile_count, slot_count),
        in_specs=[
            pl.BlockSpec((1, TILE, feat_width), lambda i, j, s, c: (i, 0, 0)),
            pl.BlockSpec((1, TILE, 2 * feat_width), kv_map),
        ],
        out_specs=pl.BlockSpec((1, TILE, feat_width), lambda i, j, s, c: (i, 0, 0)),
        scratch_shapes=[
            pltpu.VMEM((HEADS, TILE, slot_count * TILE), jnp.float32),
            pltpu.VMEM((slot_count * TILE, feat_width), jnp.bfloat16),
        ],
    )
    return pl.pallas_call(
        attention_kernel,
        grid_spec=grid_spec,
        out_shape=jax.ShapeDtypeStruct(query_tiles.shape, jnp.bfloat16),
        compiler_params=pltpu.CompilerParams(
            dimension_semantics=("arbitrary", "arbitrary"),
        ),
    )(slots, counts, query_tiles, window)


def local(
    patches,
    vis_index,
    kv_list,
    kv_count,
    global_tiles,
    frame_table,
    space_table,
    ln_gain,
    ln_bias,
    w_qkv,
    w_out,
):
    tok_rows = patches.shape[0]
    feat_width = patches.shape[1]
    tile_count = tok_rows // TILE
    fsdp_size = lax.axis_size("fsdp")
    seq_size = lax.axis_size("seq")
    seq_at = lax.axis_index("seq")
    group_tiles = tile_count * fsdp_size

    stream = embed(patches, vis_index, frame_table, space_table)

    normed = layer_norm(stream, ln_gain, ln_bias)
    group_rows = lax.all_gather(normed, "fsdp", axis=0, tiled=True).reshape(
        group_tiles, TILE, feat_width
    )
    w_src, group_rows = lax.optimization_barrier((w_qkv, group_rows))
    w_full = gathered_weight(w_src)

    global_ids = global_tiles.astype(jnp.int32)
    global_rows = group_rows[global_ids % group_tiles]
    owners = global_ids // group_tiles
    for bit in sorted(range(seq_size.bit_length() - 1), key=lambda b: -b):
        step = 1 << bit
        held = ((seq_at ^ owners) & (2 * step - 1)) == 0
        got = lax.ppermute(global_rows, "seq", [(i, i ^ step) for i in range(seq_size)])
        global_rows = jnp.where(held[:, None, None], global_rows, got)
    near_blocks = []
    near_rank = []
    for reach in REACH:
        picks, rank = near_tiles(kv_list, seq_at + reach, group_tiles)
        asked = passed_along(picks, "seq", reach)
        near_blocks.append(passed_along(group_rows[asked], "seq", -reach))
        near_rank.append(rank)
    window_rows = jnp.concatenate(
        [group_rows] + near_blocks + [global_rows], axis=0
    )
    window = jnp.dot(
        window_rows.reshape(-1, feat_width), w_full[:, feat_width:],
        preferred_element_type=jnp.float32,
    ).astype(jnp.bfloat16).reshape(-1, TILE, 2 * feat_width)
    query = jnp.dot(
        normed, w_full[:, :feat_width], preferred_element_type=jnp.float32
    ).astype(jnp.bfloat16)
    near_rank = jnp.stack(near_rank)

    entry_group = kv_list // group_tiles
    entry_local = kv_list % group_tiles
    reach_of = entry_group - seq_at
    reach_slot = jnp.where(reach_of < 0, reach_of + 2, reach_of + 1)
    reach_slot = jnp.clip(reach_slot, 0, len(REACH) - 1)
    entry_rank = near_rank[reach_slot, entry_local]
    local_lists = jnp.where(
        reach_of == 0, entry_local, group_tiles + NEAR * reach_slot + jnp.clip(entry_rank, 0, NEAR - 1)
    )
    global_slots = group_tiles + NEAR * len(REACH) + jnp.arange(GLOBAL, dtype=jnp.int32)

    query_tiles = query.reshape(tile_count, TILE, feat_width)
    slots = jnp.concatenate(
        [local_lists, jnp.broadcast_to(global_slots, (tile_count, GLOBAL))], axis=1
    ).astype(jnp.int32)
    heads_out = attend(query_tiles, window, slots, kv_count).reshape(tok_rows, feat_width)
    return jnp.dot(
        heads_out,
        lax.all_gather(w_out, "fsdp", axis=0, tiled=True),
        preferred_element_type=jnp.float32,
    ).astype(jnp.bfloat16)


def solution(mesh):
    return jax.shard_map(
        local,
        mesh=mesh,
        in_specs=(
            P(("seq", "fsdp"), None),
            P(("seq", "fsdp")),
            P(("seq", "fsdp"), None),
            P(("seq", "fsdp")),
            P(),
            P(),
            P(),
            P(),
            P(),
            P("fsdp", None),
            P("fsdp", None),
        ),
        out_specs=P(("seq", "fsdp"), None),
        check_vma=False,
    )
```

```python
import jax
import jax.numpy as jnp
from jax import lax
from jax.experimental import pallas as pl
from jax.experimental.pallas import tpu as pltpu
from jax.sharding import PartitionSpec as P

HEADS = 16
TILE = 128
KT = 16
GLOBAL = 2
PATCHES = 512
NEAR = 3
REACH = (-2, -1, 1, 2)


def passed_along(block, axis, distance):
    devices = range(lax.axis_size(axis))
    route = [(i - distance, i) for i in devices if i - distance in devices]
    return lax.ppermute(block, axis, route)


def gathered_weight(shard):
    core = lax.axis_index("seq") % 2
    half = shard.shape[1] // 2
    mine = lax.all_gather(
        lax.dynamic_slice_in_dim(shard, core * half, half, 1), "fsdp", axis=0, tiled=True
    )
    seq_size = lax.axis_size("seq")
    other = lax.ppermute(mine, "seq", [(i, i ^ 1) for i in range(seq_size)])
    low = jnp.where(core == 0, mine, other)
    high = jnp.where(core == 0, other, mine)
    return jnp.concatenate([low, high], axis=1)


def layer_norm(stream, ln_gain, ln_bias):
    stream32 = stream.astype(jnp.float32)
    mean_val = jnp.mean(stream32, axis=-1, keepdims=True)
    centred = stream32 - mean_val
    variance = jnp.mean(centred * centred, axis=-1, keepdims=True)
    scaled = centred * lax.rsqrt(variance + 1e-06)
    return (scaled * ln_gain.astype(jnp.float32) + ln_bias.astype(jnp.float32)).astype(jnp.bfloat16)


def embed(patches, vis_index, frame_table, space_table):
    frame_ids = vis_index // PATCHES
    patch_ids = vis_index % PATCHES
    return (
        patches.astype(jnp.float32)
        + frame_table[frame_ids].astype(jnp.float32)
        + space_table[patch_ids].astype(jnp.float32)
    ).astype(jnp.bfloat16)


def near_tiles(entries, group, group_tiles):
    cand = group * group_tiles + jnp.arange(group_tiles, dtype=jnp.int32)
    named = jnp.any(entries.reshape(-1, 1) == cand[None, :], axis=0)
    rank = jnp.cumsum(named.astype(jnp.int32)) - 1
    local_ids = jnp.arange(group_tiles, dtype=jnp.int32)
    picks = jnp.stack(
        [jnp.sum(jnp.where(named & (rank == j), local_ids, 0)) for j in range(NEAR)]
    )
    return picks, rank


def attention_kernel(slots_ref, counts_ref, q_ref, kv_ref, o_ref, s_scr, v_scr):
    tile_at = pl.program_id(0)
    slot_at = pl.program_id(1)
    slot_count = KT + GLOBAL
    feat_width = q_ref.shape[-1]
    head_size = feat_width // HEADS
    live_count = counts_ref[tile_at]
    live = (slot_at >= KT) | (slot_at < live_count)
    key_at = pl.multiple_of(slot_at * TILE, TILE)

    @pl.when(live)
    def _():
        for head in range(HEADS):
            cols = slice(head * head_size, (head + 1) * head_size)
            scores = lax.dot_general(
                q_ref[0, :, cols], kv_ref[0, :, cols], (((1,), (1,)), ((), ())),
                preferred_element_type=jnp.float32,
            )
            s_scr[head, :, pl.ds(key_at, TILE)] = scores * head_size ** (-0.5)
        v_scr[pl.ds(key_at, TILE), :] = kv_ref[0, :, feat_width:]

    @pl.when(jnp.logical_not(live))
    def _():
        v_scr[pl.ds(key_at, TILE), :] = jnp.zeros((TILE, feat_width), v_scr.dtype)

    @pl.when(slot_at == slot_count - 1)
    def _():
        key_slot = lax.broadcasted_iota(jnp.int32, (TILE, slot_count * TILE), 1) // TILE
        key_live = (key_slot >= KT) | (key_slot < live_count)
        for head in range(HEADS):
            cols = slice(head * head_size, (head + 1) * head_size)
            scores = jnp.where(key_live, s_scr[head], -jnp.inf)
            row_max = jnp.max(scores, axis=-1, keepdims=True)
            weights_raw = jnp.exp(scores - row_max)
            probs = (weights_raw / jnp.sum(weights_raw, axis=-1, keepdims=True)).astype(jnp.bfloat16)
            mixed = jnp.dot(probs, v_scr[:, cols], preferred_element_type=jnp.float32)
            o_ref[0, :, cols] = mixed.astype(o_ref.dtype)


def attend(query_tiles, window, slots, counts):
    tile_count, _, feat_width = query_tiles.shape
    slot_count = KT + GLOBAL

    def kv_map(i, j, slots_ref, counts_ref):
        live_count = counts_ref[i]
        fetch = jnp.where((j >= KT) | (j < live_count), j, jnp.maximum(live_count - 1, 0))
        return (slots_ref[i, fetch], 0, 0)

    grid_spec = pltpu.PrefetchScalarGridSpec(
        num_scalar_prefetch=2,
        grid=(tile_count, slot_count),
        in_specs=[
            pl.BlockSpec((1, TILE, feat_width), lambda i, j, s, c: (i, 0, 0)),
            pl.BlockSpec((1, TILE, 2 * feat_width), kv_map),
        ],
        out_specs=pl.BlockSpec((1, TILE, feat_width), lambda i, j, s, c: (i, 0, 0)),
        scratch_shapes=[
            pltpu.VMEM((HEADS, TILE, slot_count * TILE), jnp.float32),
            pltpu.VMEM((slot_count * TILE, feat_width), jnp.bfloat16),
        ],
    )
    return pl.pallas_call(
        attention_kernel,
        grid_spec=grid_spec,
        out_shape=jax.ShapeDtypeStruct(query_tiles.shape, jnp.bfloat16),
        compiler_params=pltpu.CompilerParams(
            dimension_semantics=("arbitrary", "arbitrary"),
        ),
    )(slots, counts, query_tiles, window)


def local(
    patches,
    vis_index,
    kv_list,
    kv_count,
    global_tiles,
    frame_table,
    space_table,
    ln_gain,
    ln_bias,
    w_qkv,
    w_out,
):
    tok_rows = patches.shape[0]
    feat_width = patches.shape[1]
    tile_count = tok_rows // TILE
    fsdp_size = lax.axis_size("fsdp")
    seq_size = lax.axis_size("seq")
    seq_at = lax.axis_index("seq")
    group_tiles = tile_count * fsdp_size

    stream = embed(patches, vis_index, frame_table, space_table)

    normed = layer_norm(stream, ln_gain, ln_bias)
    group_rows = lax.all_gather(normed, "fsdp", axis=0, tiled=True).reshape(
        group_tiles, TILE, feat_width
    )
    w_src, group_rows = lax.optimization_barrier((w_qkv, group_rows))
    w_full = gathered_weight(w_src)

    dev_count = seq_size * fsdp_size
    dev_at = seq_at * fsdp_size + lax.axis_index("fsdp")
    global_ids = global_tiles.astype(jnp.int32)
    global_rows = jnp.stack(
        [
            lax.dynamic_slice_in_dim(normed, global_ids[n] % tile_count * TILE, TILE, 0)
            for n in range(GLOBAL)
        ]
    )
    owners = global_ids // tile_count
    done_bits = 0
    for bit in sorted(range(dev_count.bit_length() - 1), key=lambda b: -b):
        step = 1 << bit
        held = ((dev_at ^ owners) & ~done_bits) == 0
        got = lax.ppermute(
            global_rows, ("seq", "fsdp"), [(i, i ^ step) for i in range(dev_count)]
        )
        global_rows = jnp.where(held[:, None, None], global_rows, got)
        done_bits |= step
    near_blocks = []
    near_rank = []
    for reach in REACH:
        picks, rank = near_tiles(kv_list, seq_at + reach, group_tiles)
        asked = passed_along(picks, "seq", reach)
        near_blocks.append(passed_along(group_rows[asked], "seq", -reach))
        near_rank.append(rank)
    window_rows = jnp.concatenate(
        [group_rows] + near_blocks + [global_rows], axis=0
    )
    window = jnp.dot(
        window_rows.reshape(-1, feat_width), w_full[:, feat_width:],
        preferred_element_type=jnp.float32,
    ).astype(jnp.bfloat16).reshape(-1, TILE, 2 * feat_width)
    query = jnp.dot(
        normed, w_full[:, :feat_width], preferred_element_type=jnp.float32
    ).astype(jnp.bfloat16)
    near_rank = jnp.stack(near_rank)

    entry_group = kv_list // group_tiles
    entry_local = kv_list % group_tiles
    reach_of = entry_group - seq_at
    reach_slot = jnp.where(reach_of < 0, reach_of + 2, reach_of + 1)
    reach_slot = jnp.clip(reach_slot, 0, len(REACH) - 1)
    entry_rank = near_rank[reach_slot, entry_local]
    local_lists = jnp.where(
        reach_of == 0, entry_local, group_tiles + NEAR * reach_slot + jnp.clip(entry_rank, 0, NEAR - 1)
    )
    global_slots = group_tiles + NEAR * len(REACH) + jnp.arange(GLOBAL, dtype=jnp.int32)

    query_tiles = query.reshape(tile_count, TILE, feat_width)
    slots = jnp.concatenate(
        [local_lists, jnp.broadcast_to(global_slots, (tile_count, GLOBAL))], axis=1
    ).astype(jnp.int32)
    heads_out = attend(query_tiles, window, slots, kv_count).reshape(tok_rows, feat_width)
    return jnp.dot(
        heads_out,
        lax.all_gather(w_out, "fsdp", axis=0, tiled=True),
        preferred_element_type=jnp.float32,
    ).astype(jnp.bfloat16)


def solution(mesh):
    return jax.shard_map(
        local,
        mesh=mesh,
        in_specs=(
            P(("seq", "fsdp"), None),
            P(("seq", "fsdp")),
            P(("seq", "fsdp"), None),
            P(("seq", "fsdp")),
            P(),
            P(),
            P(),
            P(),
            P(),
            P("fsdp", None),
            P("fsdp", None),
        ),
        out_specs=P(("seq", "fsdp"), None),
        check_vma=False,
    )
```

```python
import jax
import jax.numpy as jnp
from jax import lax
from jax.experimental import pallas as pl
from jax.experimental.pallas import tpu as pltpu
from jax.sharding import PartitionSpec as P

HEADS = 16
TILE = 128
KT = 16
GLOBAL = 2
PATCHES = 512
NEAR = 3
REACH = (-2, -1, 1, 2)


def passed_along(block, axis, distance):
    devices = range(lax.axis_size(axis))
    route = [(i - distance, i) for i in devices if i - distance in devices]
    return lax.ppermute(block, axis, route)


def gathered_weight(shard):
    core = lax.axis_index("seq") % 2
    half = shard.shape[1] // 2
    mine = lax.all_gather(
        lax.dynamic_slice_in_dim(shard, core * half, half, 1), "fsdp", axis=0, tiled=True
    )
    seq_size = lax.axis_size("seq")
    other = lax.ppermute(mine, "seq", [(i, i ^ 1) for i in range(seq_size)])
    low = jnp.where(core == 0, mine, other)
    high = jnp.where(core == 0, other, mine)
    return jnp.concatenate([low, high], axis=1)


def layer_norm(stream, ln_gain, ln_bias):
    stream32 = stream.astype(jnp.float32)
    mean_val = jnp.mean(stream32, axis=-1, keepdims=True)
    centred = stream32 - mean_val
    variance = jnp.mean(centred * centred, axis=-1, keepdims=True)
    scaled = centred * lax.rsqrt(variance + 1e-06)
    return (scaled * ln_gain.astype(jnp.float32) + ln_bias.astype(jnp.float32)).astype(jnp.bfloat16)


def embed(patches, vis_index, frame_table, space_table):
    frame_ids = vis_index // PATCHES
    patch_ids = vis_index % PATCHES
    return (
        patches.astype(jnp.float32)
        + frame_table[frame_ids].astype(jnp.float32)
        + space_table[patch_ids].astype(jnp.float32)
    ).astype(jnp.bfloat16)


def near_tiles(entries, group, group_tiles):
    cand = group * group_tiles + jnp.arange(group_tiles, dtype=jnp.int32)
    named = jnp.any(entries.reshape(-1, 1) == cand[None, :], axis=0)
    rank = jnp.cumsum(named.astype(jnp.int32)) - 1
    local_ids = jnp.arange(group_tiles, dtype=jnp.int32)
    picks = jnp.stack(
        [jnp.sum(jnp.where(named & (rank == j), local_ids, 0)) for j in range(NEAR)]
    )
    return picks, rank


def attention_kernel(slots_ref, counts_ref, q_ref, kv_ref, o_ref, s_scr, v_scr):
    tile_at = pl.program_id(0)
    slot_at = pl.program_id(1)
    slot_count = KT + GLOBAL
    feat_width = q_ref.shape[-1]
    head_size = feat_width // HEADS
    live_count = counts_ref[tile_at]
    live = (slot_at >= KT) | (slot_at < live_count)
    key_at = pl.multiple_of(slot_at * TILE, TILE)

    @pl.when(live)
    def _():
        for head in range(HEADS):
            cols = slice(head * head_size, (head + 1) * head_size)
            scores = lax.dot_general(
                q_ref[0, :, cols], kv_ref[0, :, cols], (((1,), (1,)), ((), ())),
                preferred_element_type=jnp.float32,
            )
            s_scr[head, :, pl.ds(key_at, TILE)] = scores * head_size ** (-0.5)
        v_scr[pl.ds(key_at, TILE), :] = kv_ref[0, :, feat_width:]

    @pl.when(jnp.logical_not(live))
    def _():
        v_scr[pl.ds(key_at, TILE), :] = jnp.zeros((TILE, feat_width), v_scr.dtype)

    @pl.when(slot_at == slot_count - 1)
    def _():
        key_slot = lax.broadcasted_iota(jnp.int32, (TILE, slot_count * TILE), 1) // TILE
        key_live = (key_slot >= KT) | (key_slot < live_count)
        for head in range(HEADS):
            cols = slice(head * head_size, (head + 1) * head_size)
            scores = jnp.where(key_live, s_scr[head], -jnp.inf)
            row_max = jnp.max(scores, axis=-1, keepdims=True)
            weights_raw = jnp.exp(scores - row_max)
            probs = (weights_raw / jnp.sum(weights_raw, axis=-1, keepdims=True)).astype(jnp.bfloat16)
            mixed = jnp.dot(probs, v_scr[:, cols], preferred_element_type=jnp.float32)
            o_ref[0, :, cols] = mixed.astype(o_ref.dtype)


def attend(query_tiles, window, slots, counts):
    tile_count, _, feat_width = query_tiles.shape
    slot_count = KT + GLOBAL

    def kv_map(i, j, slots_ref, counts_ref):
        live_count = counts_ref[i]
        fetch = jnp.where((j >= KT) | (j < live_count), j, jnp.maximum(live_count - 1, 0))
        return (slots_ref[i, fetch], 0, 0)

    grid_spec = pltpu.PrefetchScalarGridSpec(
        num_scalar_prefetch=2,
        grid=(tile_count, slot_count),
        in_specs=[
            pl.BlockSpec((1, TILE, feat_width), lambda i, j, s, c: (i, 0, 0)),
            pl.BlockSpec((1, TILE, 2 * feat_width), kv_map),
        ],
        out_specs=pl.BlockSpec((1, TILE, feat_width), lambda i, j, s, c: (i, 0, 0)),
        scratch_shapes=[
            pltpu.VMEM((HEADS, TILE, slot_count * TILE), jnp.float32),
            pltpu.VMEM((slot_count * TILE, feat_width), jnp.bfloat16),
        ],
    )
    return pl.pallas_call(
        attention_kernel,
        grid_spec=grid_spec,
        out_shape=jax.ShapeDtypeStruct(query_tiles.shape, jnp.bfloat16),
        compiler_params=pltpu.CompilerParams(
            dimension_semantics=("arbitrary", "arbitrary"),
        ),
    )(slots, counts, query_tiles, window)


def local(
    patches,
    vis_index,
    kv_list,
    kv_count,
    global_tiles,
    frame_table,
    space_table,
    ln_gain,
    ln_bias,
    w_qkv,
    w_out,
):
    tok_rows = patches.shape[0]
    feat_width = patches.shape[1]
    tile_count = tok_rows // TILE
    fsdp_size = lax.axis_size("fsdp")
    seq_size = lax.axis_size("seq")
    seq_at = lax.axis_index("seq")
    group_tiles = tile_count * fsdp_size

    stream = embed(patches, vis_index, frame_table, space_table)

    normed = layer_norm(stream, ln_gain, ln_bias)
    group_rows = lax.all_gather(normed, "fsdp", axis=0, tiled=True).reshape(
        group_tiles, TILE, feat_width
    )
    w_src, group_rows = lax.optimization_barrier((w_qkv, group_rows))
    w_full = gathered_weight(w_src)

    global_ids = global_tiles.astype(jnp.int32)
    global_rows = group_rows[global_ids % group_tiles]
    owners = global_ids // group_tiles
    seq_bits = seq_size.bit_length() - 1
    bit_order = [b for b in (1, 2) if b < seq_bits]
    bit_order += [b for b in range(seq_bits - 1, -1, -1) if b not in bit_order]
    done_bits = 0
    for bit in bit_order:
        step = 1 << bit
        held = ((seq_at ^ owners) & ~done_bits & (seq_size - 1)) == 0
        done_bits |= step
        got = lax.ppermute(global_rows, "seq", [(i, i ^ step) for i in range(seq_size)])
        global_rows = jnp.where(held[:, None, None], global_rows, got)
    near_blocks = []
    near_rank = []
    for reach in REACH:
        picks, rank = near_tiles(kv_list, seq_at + reach, group_tiles)
        asked = passed_along(picks, "seq", reach)
        near_blocks.append(passed_along(group_rows[asked], "seq", -reach))
        near_rank.append(rank)
    window_rows = jnp.concatenate(
        [group_rows] + near_blocks + [global_rows], axis=0
    )
    window = jnp.dot(
        window_rows.reshape(-1, feat_width), w_full[:, feat_width:],
        preferred_element_type=jnp.float32,
    ).astype(jnp.bfloat16).reshape(-1, TILE, 2 * feat_width)
    query = jnp.dot(
        normed, w_full[:, :feat_width], preferred_element_type=jnp.float32
    ).astype(jnp.bfloat16)
    near_rank = jnp.stack(near_rank)

    entry_group = kv_list // group_tiles
    entry_local = kv_list % group_tiles
    reach_of = entry_group - seq_at
    reach_slot = jnp.where(reach_of < 0, reach_of + 2, reach_of + 1)
    reach_slot = jnp.clip(reach_slot, 0, len(REACH) - 1)
    entry_rank = near_rank[reach_slot, entry_local]
    local_lists = jnp.where(
        reach_of == 0, entry_local, group_tiles + NEAR * reach_slot + jnp.clip(entry_rank, 0, NEAR - 1)
    )
    global_slots = group_tiles + NEAR * len(REACH) + jnp.arange(GLOBAL, dtype=jnp.int32)

    query_tiles = query.reshape(tile_count, TILE, feat_width)
    slots = jnp.concatenate(
        [local_lists, jnp.broadcast_to(global_slots, (tile_count, GLOBAL))], axis=1
    ).astype(jnp.int32)
    heads_out = attend(query_tiles, window, slots, kv_count).reshape(tok_rows, feat_width)
    return jnp.dot(
        heads_out,
        lax.all_gather(w_out, "fsdp", axis=0, tiled=True),
        preferred_element_type=jnp.float32,
    ).astype(jnp.bfloat16)


def solution(mesh):
    return jax.shard_map(
        local,
        mesh=mesh,
        in_specs=(
            P(("seq", "fsdp"), None),
            P(("seq", "fsdp")),
            P(("seq", "fsdp"), None),
            P(("seq", "fsdp")),
            P(),
            P(),
            P(),
            P(),
            P(),
            P("fsdp", None),
            P("fsdp", None),
        ),
        out_specs=P(("seq", "fsdp"), None),
        check_vma=False,
    )
```

```python
import jax
import jax.numpy as jnp
from jax import lax
from jax.experimental import pallas as pl
from jax.experimental.pallas import tpu as pltpu
from jax.sharding import PartitionSpec as P

HEADS = 16
TILE = 128
KT = 16
GLOBAL = 2
PATCHES = 512
NEAR = 3
REACH = (-2, -1, 1, 2)


def passed_along(block, axis, distance):
    devices = range(lax.axis_size(axis))
    route = [(i - distance, i) for i in devices if i - distance in devices]
    return lax.ppermute(block, axis, route)


def gathered_weight(shard):
    core = lax.axis_index("seq") % 2
    half = shard.shape[1] // 2
    mine = lax.all_gather(
        lax.dynamic_slice_in_dim(shard, core * half, half, 1), "fsdp", axis=0, tiled=True
    )
    seq_size = lax.axis_size("seq")
    other = lax.ppermute(mine, "seq", [(i, i ^ 1) for i in range(seq_size)])
    low = jnp.where(core == 0, mine, other)
    high = jnp.where(core == 0, other, mine)
    return jnp.concatenate([low, high], axis=1)


def layer_norm(stream, ln_gain, ln_bias):
    stream32 = stream.astype(jnp.float32)
    mean_val = jnp.mean(stream32, axis=-1, keepdims=True)
    centred = stream32 - mean_val
    variance = jnp.mean(centred * centred, axis=-1, keepdims=True)
    scaled = centred * lax.rsqrt(variance + 1e-06)
    return (scaled * ln_gain.astype(jnp.float32) + ln_bias.astype(jnp.float32)).astype(jnp.bfloat16)


def embed(patches, vis_index, frame_table, space_table):
    frame_ids = vis_index // PATCHES
    patch_ids = vis_index % PATCHES
    return (
        patches.astype(jnp.float32)
        + frame_table[frame_ids].astype(jnp.float32)
        + space_table[patch_ids].astype(jnp.float32)
    ).astype(jnp.bfloat16)


def near_tiles(entries, group, group_tiles):
    cand = group * group_tiles + jnp.arange(group_tiles, dtype=jnp.int32)
    named = jnp.any(entries.reshape(-1, 1) == cand[None, :], axis=0)
    rank = jnp.cumsum(named.astype(jnp.int32)) - 1
    local_ids = jnp.arange(group_tiles, dtype=jnp.int32)
    picks = jnp.stack(
        [jnp.sum(jnp.where(named & (rank == j), local_ids, 0)) for j in range(NEAR)]
    )
    return picks, rank


def attention_kernel(slots_ref, counts_ref, q_ref, kv_ref, o_ref, s_scr, v_scr):
    tile_at = pl.program_id(0)
    slot_at = pl.program_id(1)
    slot_count = KT + GLOBAL
    feat_width = q_ref.shape[-1]
    head_size = feat_width // HEADS
    live_count = counts_ref[tile_at]
    live = (slot_at >= KT) | (slot_at < live_count)
    key_at = pl.multiple_of(slot_at * TILE, TILE)

    @pl.when(live)
    def _():
        for head in range(HEADS):
            cols = slice(head * head_size, (head + 1) * head_size)
            scores = lax.dot_general(
                q_ref[0, :, cols], kv_ref[0, :, cols], (((1,), (1,)), ((), ())),
                preferred_element_type=jnp.float32,
            )
            s_scr[head, :, pl.ds(key_at, TILE)] = scores * head_size ** (-0.5)
        v_scr[pl.ds(key_at, TILE), :] = kv_ref[0, :, feat_width:]

    @pl.when(jnp.logical_not(live))
    def _():
        v_scr[pl.ds(key_at, TILE), :] = jnp.zeros((TILE, feat_width), v_scr.dtype)

    @pl.when(slot_at == slot_count - 1)
    def _():
        key_slot = lax.broadcasted_iota(jnp.int32, (TILE, slot_count * TILE), 1) // TILE
        key_live = (key_slot >= KT) | (key_slot < live_count)
        for head in range(HEADS):
            cols = slice(head * head_size, (head + 1) * head_size)
            scores = jnp.where(key_live, s_scr[head], -jnp.inf)
            row_max = jnp.max(scores, axis=-1, keepdims=True)
            weights_raw = jnp.exp(scores - row_max)
            probs = (weights_raw / jnp.sum(weights_raw, axis=-1, keepdims=True)).astype(jnp.bfloat16)
            mixed = jnp.dot(probs, v_scr[:, cols], preferred_element_type=jnp.float32)
            o_ref[0, :, cols] = mixed.astype(o_ref.dtype)


def attend(query_tiles, window, slots, counts):
    tile_count, _, feat_width = query_tiles.shape
    slot_count = KT + GLOBAL

    def kv_map(i, j, slots_ref, counts_ref):
        live_count = counts_ref[i]
        fetch = jnp.where((j >= KT) | (j < live_count), j, jnp.maximum(live_count - 1, 0))
        return (slots_ref[i, fetch], 0, 0)

    grid_spec = pltpu.PrefetchScalarGridSpec(
        num_scalar_prefetch=2,
        grid=(tile_count, slot_count),
        in_specs=[
            pl.BlockSpec((1, TILE, feat_width), lambda i, j, s, c: (i, 0, 0)),
            pl.BlockSpec((1, TILE, 2 * feat_width), kv_map),
        ],
        out_specs=pl.BlockSpec((1, TILE, feat_width), lambda i, j, s, c: (i, 0, 0)),
        scratch_shapes=[
            pltpu.VMEM((HEADS, TILE, slot_count * TILE), jnp.float32),
            pltpu.VMEM((slot_count * TILE, feat_width), jnp.bfloat16),
        ],
    )
    return pl.pallas_call(
        attention_kernel,
        grid_spec=grid_spec,
        out_shape=jax.ShapeDtypeStruct(query_tiles.shape, jnp.bfloat16),
        compiler_params=pltpu.CompilerParams(
            dimension_semantics=("arbitrary", "arbitrary"),
        ),
    )(slots, counts, query_tiles, window)


def local(
    patches,
    vis_index,
    kv_list,
    kv_count,
    global_tiles,
    frame_table,
    space_table,
    ln_gain,
    ln_bias,
    w_qkv,
    w_out,
):
    tok_rows = patches.shape[0]
    feat_width = patches.shape[1]
    tile_count = tok_rows // TILE
    fsdp_size = lax.axis_size("fsdp")
    seq_size = lax.axis_size("seq")
    seq_at = lax.axis_index("seq")
    group_tiles = tile_count * fsdp_size

    stream = embed(patches, vis_index, frame_table, space_table)

    normed = layer_norm(stream, ln_gain, ln_bias)
    group_rows = lax.all_gather(normed, "fsdp", axis=0, tiled=True).reshape(
        group_tiles, TILE, feat_width
    )
    w_src, group_rows = lax.optimization_barrier((w_qkv, group_rows))
    w_full = gathered_weight(w_src)

    global_ids = global_tiles.astype(jnp.int32)
    global_rows = group_rows[global_ids % group_tiles]
    owners = global_ids // group_tiles
    seq_bits = seq_size.bit_length() - 1
    bit_order = [b for b in (1, 2) if b < seq_bits]
    bit_order += [b for b in range(seq_bits - 1, -1, -1) if b not in bit_order]
    done_bits = 0
    for bit in bit_order:
        step = 1 << bit
        held = ((seq_at ^ owners) & ~done_bits & (seq_size - 1)) == 0
        done_bits |= step
        got = lax.ppermute(global_rows, "seq", [(i, i ^ step) for i in range(seq_size)])
        global_rows = jnp.where(held[:, None, None], global_rows, got)
    near_blocks = []
    near_rank = []
    asked = []
    for reach in REACH:
        picks, rank = near_tiles(kv_list, seq_at + reach, group_tiles)
        asked.append(passed_along(picks, "seq", reach))
        near_rank.append(rank)
    asked, group_rows = lax.optimization_barrier((asked, group_rows))
    for reach, ids in zip(REACH, asked):
        near_blocks.append(passed_along(group_rows[ids], "seq", -reach))
    window_rows = jnp.concatenate(
        [group_rows] + near_blocks + [global_rows], axis=0
    )
    window = jnp.dot(
        window_rows.reshape(-1, feat_width), w_full[:, feat_width:],
        preferred_element_type=jnp.float32,
    ).astype(jnp.bfloat16).reshape(-1, TILE, 2 * feat_width)
    query = jnp.dot(
        normed, w_full[:, :feat_width], preferred_element_type=jnp.float32
    ).astype(jnp.bfloat16)
    near_rank = jnp.stack(near_rank)

    entry_group = kv_list // group_tiles
    entry_local = kv_list % group_tiles
    reach_of = entry_group - seq_at
    reach_slot = jnp.where(reach_of < 0, reach_of + 2, reach_of + 1)
    reach_slot = jnp.clip(reach_slot, 0, len(REACH) - 1)
    entry_rank = near_rank[reach_slot, entry_local]
    local_lists = jnp.where(
        reach_of == 0, entry_local, group_tiles + NEAR * reach_slot + jnp.clip(entry_rank, 0, NEAR - 1)
    )
    global_slots = group_tiles + NEAR * len(REACH) + jnp.arange(GLOBAL, dtype=jnp.int32)

    query_tiles = query.reshape(tile_count, TILE, feat_width)
    slots = jnp.concatenate(
        [local_lists, jnp.broadcast_to(global_slots, (tile_count, GLOBAL))], axis=1
    ).astype(jnp.int32)
    heads_out = attend(query_tiles, window, slots, kv_count).reshape(tok_rows, feat_width)
    return jnp.dot(
        heads_out,
        lax.all_gather(w_out, "fsdp", axis=0, tiled=True),
        preferred_element_type=jnp.float32,
    ).astype(jnp.bfloat16)


def solution(mesh):
    return jax.shard_map(
        local,
        mesh=mesh,
        in_specs=(
            P(("seq", "fsdp"), None),
            P(("seq", "fsdp")),
            P(("seq", "fsdp"), None),
            P(("seq", "fsdp")),
            P(),
            P(),
            P(),
            P(),
            P(),
            P("fsdp", None),
            P("fsdp", None),
        ),
        out_specs=P(("seq", "fsdp"), None),
        check_vma=False,
    )
```

```python
import jax
import jax.numpy as jnp
from jax import lax
from jax.experimental import pallas as pl
from jax.experimental.pallas import tpu as pltpu
from jax.sharding import PartitionSpec as P

HEADS = 16
TILE = 128
KT = 16
GLOBAL = 2
PATCHES = 512
NEAR = 3
REACH = (-2, -1, 1, 2)


def passed_along(block, axis, distance):
    devices = range(lax.axis_size(axis))
    route = [(i - distance, i) for i in devices if i - distance in devices]
    return lax.ppermute(block, axis, route)


def gathered_weight(shard):
    core = lax.axis_index("seq") % 2
    half = shard.shape[1] // 2
    mine = lax.all_gather(
        lax.dynamic_slice_in_dim(shard, core * half, half, 1), "fsdp", axis=0, tiled=True
    )
    seq_size = lax.axis_size("seq")
    other = lax.ppermute(mine, "seq", [(i, i ^ 1) for i in range(seq_size)])
    low = jnp.where(core == 0, mine, other)
    high = jnp.where(core == 0, other, mine)
    return jnp.concatenate([low, high], axis=1)


def layer_norm(stream, ln_gain, ln_bias):
    stream32 = stream.astype(jnp.float32)
    mean_val = jnp.mean(stream32, axis=-1, keepdims=True)
    centred = stream32 - mean_val
    variance = jnp.mean(centred * centred, axis=-1, keepdims=True)
    scaled = centred * lax.rsqrt(variance + 1e-06)
    return (scaled * ln_gain.astype(jnp.float32) + ln_bias.astype(jnp.float32)).astype(jnp.bfloat16)


def embed(patches, vis_index, frame_table, space_table):
    frame_ids = vis_index // PATCHES
    patch_ids = vis_index % PATCHES
    return (
        patches.astype(jnp.float32)
        + frame_table[frame_ids].astype(jnp.float32)
        + space_table[patch_ids].astype(jnp.float32)
    ).astype(jnp.bfloat16)


def near_tiles(entries, group, group_tiles):
    cand = group * group_tiles + jnp.arange(group_tiles, dtype=jnp.int32)
    named = jnp.any(entries.reshape(-1, 1) == cand[None, :], axis=0)
    rank = jnp.cumsum(named.astype(jnp.int32)) - 1
    local_ids = jnp.arange(group_tiles, dtype=jnp.int32)
    picks = jnp.stack(
        [jnp.sum(jnp.where(named & (rank == j), local_ids, 0)) for j in range(NEAR)]
    )
    return picks, rank


def attention_kernel(slots_ref, counts_ref, q_ref, kv_ref, o_ref, s_scr, v_scr):
    tile_at = pl.program_id(0)
    slot_at = pl.program_id(1)
    slot_count = KT + GLOBAL
    feat_width = q_ref.shape[-1]
    head_size = feat_width // HEADS
    live_count = counts_ref[tile_at]
    live = (slot_at >= KT) | (slot_at < live_count)
    key_at = pl.multiple_of(slot_at * TILE, TILE)

    @pl.when(live)
    def _():
        for head in range(HEADS):
            cols = slice(head * head_size, (head + 1) * head_size)
            scores = lax.dot_general(
                q_ref[0, :, cols], kv_ref[0, :, cols], (((1,), (1,)), ((), ())),
                preferred_element_type=jnp.float32,
            )
            s_scr[head, :, pl.ds(key_at, TILE)] = scores * head_size ** (-0.5)
        v_scr[pl.ds(key_at, TILE), :] = kv_ref[0, :, feat_width:]

    @pl.when(jnp.logical_not(live))
    def _():
        v_scr[pl.ds(key_at, TILE), :] = jnp.zeros((TILE, feat_width), v_scr.dtype)

    @pl.when(slot_at == slot_count - 1)
    def _():
        key_slot = lax.broadcasted_iota(jnp.int32, (TILE, slot_count * TILE), 1) // TILE
        key_live = (key_slot >= KT) | (key_slot < live_count)
        for head in range(HEADS):
            cols = slice(head * head_size, (head + 1) * head_size)
            scores = jnp.where(key_live, s_scr[head], -jnp.inf)
            row_max = jnp.max(scores, axis=-1, keepdims=True)
            weights_raw = jnp.exp(scores - row_max)
            probs = (weights_raw / jnp.sum(weights_raw, axis=-1, keepdims=True)).astype(jnp.bfloat16)
            mixed = jnp.dot(probs, v_scr[:, cols], preferred_element_type=jnp.float32)
            o_ref[0, :, cols] = mixed.astype(o_ref.dtype)


def attend(query_tiles, window, slots, counts):
    tile_count, _, feat_width = query_tiles.shape
    slot_count = KT + GLOBAL

    def kv_map(i, j, slots_ref, counts_ref):
        live_count = counts_ref[i]
        fetch = jnp.where((j >= KT) | (j < live_count), j, jnp.maximum(live_count - 1, 0))
        return (slots_ref[i, fetch], 0, 0)

    grid_spec = pltpu.PrefetchScalarGridSpec(
        num_scalar_prefetch=2,
        grid=(tile_count, slot_count),
        in_specs=[
            pl.BlockSpec((1, TILE, feat_width), lambda i, j, s, c: (i, 0, 0)),
            pl.BlockSpec((1, TILE, 2 * feat_width), kv_map),
        ],
        out_specs=pl.BlockSpec((1, TILE, feat_width), lambda i, j, s, c: (i, 0, 0)),
        scratch_shapes=[
            pltpu.VMEM((HEADS, TILE, slot_count * TILE), jnp.float32),
            pltpu.VMEM((slot_count * TILE, feat_width), jnp.bfloat16),
        ],
    )
    return pl.pallas_call(
        attention_kernel,
        grid_spec=grid_spec,
        out_shape=jax.ShapeDtypeStruct(query_tiles.shape, jnp.bfloat16),
        compiler_params=pltpu.CompilerParams(
            dimension_semantics=("arbitrary", "arbitrary"),
        ),
    )(slots, counts, query_tiles, window)


def local(
    patches,
    vis_index,
    kv_list,
    kv_count,
    global_tiles,
    frame_table,
    space_table,
    ln_gain,
    ln_bias,
    w_qkv,
    w_out,
):
    tok_rows = patches.shape[0]
    feat_width = patches.shape[1]
    tile_count = tok_rows // TILE
    fsdp_size = lax.axis_size("fsdp")
    seq_size = lax.axis_size("seq")
    seq_at = lax.axis_index("seq")
    group_tiles = tile_count * fsdp_size

    stream = embed(patches, vis_index, frame_table, space_table)

    normed = layer_norm(stream, ln_gain, ln_bias)
    group_rows = lax.all_gather(normed, "fsdp", axis=0, tiled=True).reshape(
        group_tiles, TILE, feat_width
    )
    w_src, group_rows = lax.optimization_barrier((w_qkv, group_rows))
    w_full = gathered_weight(w_src)

    global_ids = global_tiles.astype(jnp.int32)
    global_rows = group_rows[global_ids % group_tiles]
    owners = global_ids // group_tiles
    seq_bits = seq_size.bit_length() - 1
    bit_order = [b for b in (1, 2) if b < seq_bits]
    bit_order += [b for b in range(seq_bits - 1, -1, -1) if b not in bit_order]
    done_bits = 0
    for stage, bit in enumerate(bit_order):
        if stage == 3:
            w_full, global_rows = lax.optimization_barrier((w_full, global_rows))
        step = 1 << bit
        held = ((seq_at ^ owners) & ~done_bits & (seq_size - 1)) == 0
        done_bits |= step
        got = lax.ppermute(global_rows, "seq", [(i, i ^ step) for i in range(seq_size)])
        global_rows = jnp.where(held[:, None, None], global_rows, got)
    near_blocks = []
    near_rank = []
    for reach in REACH:
        picks, rank = near_tiles(kv_list, seq_at + reach, group_tiles)
        asked = passed_along(picks, "seq", reach)
        near_blocks.append(passed_along(group_rows[asked], "seq", -reach))
        near_rank.append(rank)
    window_rows = jnp.concatenate(
        [group_rows] + near_blocks + [global_rows], axis=0
    )
    window = jnp.dot(
        window_rows.reshape(-1, feat_width), w_full[:, feat_width:],
        preferred_element_type=jnp.float32,
    ).astype(jnp.bfloat16).reshape(-1, TILE, 2 * feat_width)
    query = jnp.dot(
        normed, w_full[:, :feat_width], preferred_element_type=jnp.float32
    ).astype(jnp.bfloat16)
    near_rank = jnp.stack(near_rank)

    entry_group = kv_list // group_tiles
    entry_local = kv_list % group_tiles
    reach_of = entry_group - seq_at
    reach_slot = jnp.where(reach_of < 0, reach_of + 2, reach_of + 1)
    reach_slot = jnp.clip(reach_slot, 0, len(REACH) - 1)
    entry_rank = near_rank[reach_slot, entry_local]
    local_lists = jnp.where(
        reach_of == 0, entry_local, group_tiles + NEAR * reach_slot + jnp.clip(entry_rank, 0, NEAR - 1)
    )
    global_slots = group_tiles + NEAR * len(REACH) + jnp.arange(GLOBAL, dtype=jnp.int32)

    query_tiles = query.reshape(tile_count, TILE, feat_width)
    slots = jnp.concatenate(
        [local_lists, jnp.broadcast_to(global_slots, (tile_count, GLOBAL))], axis=1
    ).astype(jnp.int32)
    heads_out = attend(query_tiles, window, slots, kv_count).reshape(tok_rows, feat_width)
    return jnp.dot(
        heads_out,
        lax.all_gather(w_out, "fsdp", axis=0, tiled=True),
        preferred_element_type=jnp.float32,
    ).astype(jnp.bfloat16)


def solution(mesh):
    return jax.shard_map(
        local,
        mesh=mesh,
        in_specs=(
            P(("seq", "fsdp"), None),
            P(("seq", "fsdp")),
            P(("seq", "fsdp"), None),
            P(("seq", "fsdp")),
            P(),
            P(),
            P(),
            P(),
            P(),
            P("fsdp", None),
            P("fsdp", None),
        ),
        out_specs=P(("seq", "fsdp"), None),
        check_vma=False,
    )
```

```python
import jax
import jax.numpy as jnp
from jax import lax
from jax.experimental import pallas as pl
from jax.experimental.pallas import tpu as pltpu
from jax.sharding import PartitionSpec as P

HEADS = 16
TILE = 128
KT = 16
GLOBAL = 2
PATCHES = 512
NEAR = 3
REACH = (-2, -1, 1, 2)


def passed_along(block, axis, distance):
    devices = range(lax.axis_size(axis))
    route = [(i - distance, i) for i in devices if i - distance in devices]
    return lax.ppermute(block, axis, route)


def gathered_weight(shard):
    core = lax.axis_index("seq") % 2
    half = shard.shape[1] // 2
    mine = lax.all_gather(
        lax.dynamic_slice_in_dim(shard, core * half, half, 1), "fsdp", axis=0, tiled=True
    )
    seq_size = lax.axis_size("seq")
    other = lax.ppermute(mine, "seq", [(i, i ^ 1) for i in range(seq_size)])
    low = jnp.where(core == 0, mine, other)
    high = jnp.where(core == 0, other, mine)
    return jnp.concatenate([low, high], axis=1)


def layer_norm(stream, ln_gain, ln_bias):
    stream32 = stream.astype(jnp.float32)
    mean_val = jnp.mean(stream32, axis=-1, keepdims=True)
    centred = stream32 - mean_val
    variance = jnp.mean(centred * centred, axis=-1, keepdims=True)
    scaled = centred * lax.rsqrt(variance + 1e-06)
    return (scaled * ln_gain.astype(jnp.float32) + ln_bias.astype(jnp.float32)).astype(jnp.bfloat16)


def embed(patches, vis_index, frame_table, space_table):
    frame_ids = vis_index // PATCHES
    patch_ids = vis_index % PATCHES
    return (
        patches.astype(jnp.float32)
        + frame_table[frame_ids].astype(jnp.float32)
        + space_table[patch_ids].astype(jnp.float32)
    ).astype(jnp.bfloat16)


def near_tiles(entries, group, group_tiles):
    cand = group * group_tiles + jnp.arange(group_tiles, dtype=jnp.int32)
    named = jnp.any(entries.reshape(-1, 1) == cand[None, :], axis=0)
    rank = jnp.cumsum(named.astype(jnp.int32)) - 1
    local_ids = jnp.arange(group_tiles, dtype=jnp.int32)
    picks = jnp.stack(
        [jnp.sum(jnp.where(named & (rank == j), local_ids, 0)) for j in range(NEAR)]
    )
    return picks, rank


def attention_kernel(slots_ref, counts_ref, q_ref, kv_ref, o_ref, s_scr, v_scr):
    tile_at = pl.program_id(0)
    slot_at = pl.program_id(1)
    slot_count = KT + GLOBAL
    head_size = q_ref.shape[-1]
    feat_width = head_size * HEADS
    live_count = counts_ref[tile_at]
    live = (slot_at >= KT) | (slot_at < live_count)
    key_at = pl.multiple_of(slot_at * TILE, TILE)

    @pl.when(live)
    def _():
        for head in range(HEADS):
            cols = slice(head * head_size, (head + 1) * head_size)
            scores = lax.dot_general(
                q_ref[0, head], kv_ref[0, :, cols], (((1,), (1,)), ((), ())),
                preferred_element_type=jnp.float32,
            )
            s_scr[head, :, pl.ds(key_at, TILE)] = scores * head_size ** (-0.5)
        v_scr[pl.ds(key_at, TILE), :] = kv_ref[0, :, feat_width:]

    @pl.when(jnp.logical_not(live))
    def _():
        v_scr[pl.ds(key_at, TILE), :] = jnp.zeros((TILE, feat_width), v_scr.dtype)

    @pl.when(slot_at == slot_count - 1)
    def _():
        key_slot = lax.broadcasted_iota(jnp.int32, (TILE, slot_count * TILE), 1) // TILE
        key_live = (key_slot >= KT) | (key_slot < live_count)
        for head in range(HEADS):
            cols = slice(head * head_size, (head + 1) * head_size)
            scores = jnp.where(key_live, s_scr[head], -jnp.inf)
            row_max = jnp.max(scores, axis=-1, keepdims=True)
            weights_raw = jnp.exp(scores - row_max)
            probs = (weights_raw / jnp.sum(weights_raw, axis=-1, keepdims=True)).astype(jnp.bfloat16)
            mixed = jnp.dot(probs, v_scr[:, cols], preferred_element_type=jnp.float32)
            o_ref[0, :, cols] = mixed.astype(o_ref.dtype)


def attend(query_tiles, window, slots, counts):
    tile_count, _, feat_width = query_tiles.shape
    slot_count = KT + GLOBAL
    head_size = feat_width // HEADS
    query_heads = query_tiles.reshape(tile_count, TILE, HEADS, head_size).transpose(0, 2, 1, 3)

    def kv_map(i, j, slots_ref, counts_ref):
        live_count = counts_ref[i]
        fetch = jnp.where((j >= KT) | (j < live_count), j, jnp.maximum(live_count - 1, 0))
        return (slots_ref[i, fetch], 0, 0)

    grid_spec = pltpu.PrefetchScalarGridSpec(
        num_scalar_prefetch=2,
        grid=(tile_count, slot_count),
        in_specs=[
            pl.BlockSpec((1, HEADS, TILE, head_size), lambda i, j, s, c: (i, 0, 0, 0)),
            pl.BlockSpec((1, TILE, 2 * feat_width), kv_map),
        ],
        out_specs=pl.BlockSpec((1, TILE, feat_width), lambda i, j, s, c: (i, 0, 0)),
        scratch_shapes=[
            pltpu.VMEM((HEADS, TILE, slot_count * TILE), jnp.float32),
            pltpu.VMEM((slot_count * TILE, feat_width), jnp.bfloat16),
        ],
    )
    return pl.pallas_call(
        attention_kernel,
        grid_spec=grid_spec,
        out_shape=jax.ShapeDtypeStruct(query_tiles.shape, jnp.bfloat16),
        compiler_params=pltpu.CompilerParams(
            dimension_semantics=("arbitrary", "arbitrary"),
        ),
    )(slots, counts, query_heads, window)


def local(
    patches,
    vis_index,
    kv_list,
    kv_count,
    global_tiles,
    frame_table,
    space_table,
    ln_gain,
    ln_bias,
    w_qkv,
    w_out,
):
    tok_rows = patches.shape[0]
    feat_width = patches.shape[1]
    tile_count = tok_rows // TILE
    fsdp_size = lax.axis_size("fsdp")
    seq_size = lax.axis_size("seq")
    seq_at = lax.axis_index("seq")
    group_tiles = tile_count * fsdp_size

    stream = embed(patches, vis_index, frame_table, space_table)

    normed = layer_norm(stream, ln_gain, ln_bias)
    group_rows = lax.all_gather(normed, "fsdp", axis=0, tiled=True).reshape(
        group_tiles, TILE, feat_width
    )
    w_src, group_rows = lax.optimization_barrier((w_qkv, group_rows))
    w_full = gathered_weight(w_src)

    global_ids = global_tiles.astype(jnp.int32)
    global_rows = group_rows[global_ids % group_tiles]
    owners = global_ids // group_tiles
    seq_bits = seq_size.bit_length() - 1
    bit_order = [b for b in (1, 2) if b < seq_bits]
    bit_order += [b for b in range(seq_bits - 1, -1, -1) if b not in bit_order]
    done_bits = 0
    for bit in bit_order:
        step = 1 << bit
        held = ((seq_at ^ owners) & ~done_bits & (seq_size - 1)) == 0
        done_bits |= step
        got = lax.ppermute(global_rows, "seq", [(i, i ^ step) for i in range(seq_size)])
        global_rows = jnp.where(held[:, None, None], global_rows, got)
    near_blocks = []
    near_rank = []
    for reach in REACH:
        picks, rank = near_tiles(kv_list, seq_at + reach, group_tiles)
        asked = passed_along(picks, "seq", reach)
        near_blocks.append(passed_along(group_rows[asked], "seq", -reach))
        near_rank.append(rank)
    window_rows = jnp.concatenate(
        [group_rows] + near_blocks + [global_rows], axis=0
    )
    window = jnp.dot(
        window_rows.reshape(-1, feat_width), w_full[:, feat_width:],
        preferred_element_type=jnp.float32,
    ).astype(jnp.bfloat16).reshape(-1, TILE, 2 * feat_width)
    query = jnp.dot(
        normed, w_full[:, :feat_width], preferred_element_type=jnp.float32
    ).astype(jnp.bfloat16)
    near_rank = jnp.stack(near_rank)

    entry_group = kv_list // group_tiles
    entry_local = kv_list % group_tiles
    reach_of = entry_group - seq_at
    reach_slot = jnp.where(reach_of < 0, reach_of + 2, reach_of + 1)
    reach_slot = jnp.clip(reach_slot, 0, len(REACH) - 1)
    entry_rank = near_rank[reach_slot, entry_local]
    local_lists = jnp.where(
        reach_of == 0, entry_local, group_tiles + NEAR * reach_slot + jnp.clip(entry_rank, 0, NEAR - 1)
    )
    global_slots = group_tiles + NEAR * len(REACH) + jnp.arange(GLOBAL, dtype=jnp.int32)

    query_tiles = query.reshape(tile_count, TILE, feat_width)
    slots = jnp.concatenate(
        [local_lists, jnp.broadcast_to(global_slots, (tile_count, GLOBAL))], axis=1
    ).astype(jnp.int32)
    heads_out = attend(query_tiles, window, slots, kv_count).reshape(tok_rows, feat_width)
    return jnp.dot(
        heads_out,
        lax.all_gather(w_out, "fsdp", axis=0, tiled=True),
        preferred_element_type=jnp.float32,
    ).astype(jnp.bfloat16)


def solution(mesh):
    return jax.shard_map(
        local,
        mesh=mesh,
        in_specs=(
            P(("seq", "fsdp"), None),
            P(("seq", "fsdp")),
            P(("seq", "fsdp"), None),
            P(("seq", "fsdp")),
            P(),
            P(),
            P(),
            P(),
            P(),
            P("fsdp", None),
            P("fsdp", None),
        ),
        out_specs=P(("seq", "fsdp"), None),
        check_vma=False,
    )
```

```python
import jax
import jax.numpy as jnp
from jax import lax
from jax.experimental import pallas as pl
from jax.experimental.pallas import tpu as pltpu
from jax.sharding import PartitionSpec as P

HEADS = 16
TILE = 128
KT = 16
GLOBAL = 2
PATCHES = 512
NEAR = 3
REACH = (-2, -1, 1, 2)


def passed_along(block, axis, distance):
    devices = range(lax.axis_size(axis))
    route = [(i - distance, i) for i in devices if i - distance in devices]
    return lax.ppermute(block, axis, route)


def gathered_weight(shard):
    core = lax.axis_index("seq") % 2
    half = shard.shape[1] // 2
    mine = lax.all_gather(
        lax.dynamic_slice_in_dim(shard, core * half, half, 1), "fsdp", axis=0, tiled=True
    )
    seq_size = lax.axis_size("seq")
    other = lax.ppermute(mine, "seq", [(i, i ^ 1) for i in range(seq_size)])
    low = jnp.where(core == 0, mine, other)
    high = jnp.where(core == 0, other, mine)
    return jnp.concatenate([low, high], axis=1)


def layer_norm(stream, ln_gain, ln_bias):
    stream32 = stream.astype(jnp.float32)
    mean_val = jnp.mean(stream32, axis=-1, keepdims=True)
    centred = stream32 - mean_val
    variance = jnp.mean(centred * centred, axis=-1, keepdims=True)
    scaled = centred * lax.rsqrt(variance + 1e-06)
    return (scaled * ln_gain.astype(jnp.float32) + ln_bias.astype(jnp.float32)).astype(jnp.bfloat16)


def embed(patches, vis_index, frame_table, space_table):
    frame_ids = vis_index // PATCHES
    patch_ids = vis_index % PATCHES
    return (
        patches.astype(jnp.float32)
        + frame_table[frame_ids].astype(jnp.float32)
        + space_table[patch_ids].astype(jnp.float32)
    ).astype(jnp.bfloat16)


def near_tiles(entries, group, group_tiles):
    cand = group * group_tiles + jnp.arange(group_tiles, dtype=jnp.int32)
    named = jnp.any(entries.reshape(-1, 1) == cand[None, :], axis=0)
    rank = jnp.cumsum(named.astype(jnp.int32)) - 1
    local_ids = jnp.arange(group_tiles, dtype=jnp.int32)
    picks = jnp.stack(
        [jnp.sum(jnp.where(named & (rank == j), local_ids, 0)) for j in range(NEAR)]
    )
    return picks, rank


def attention_kernel(slots_ref, counts_ref, q_ref, kv_ref, o_ref, s_scr, v_scr):
    tile_at = pl.program_id(0)
    slot_at = pl.program_id(1)
    slot_count = KT + GLOBAL
    head_size = q_ref.shape[-1]
    feat_width = head_size * HEADS
    live_count = counts_ref[tile_at]
    live = (slot_at >= KT) | (slot_at < live_count)
    key_at = pl.multiple_of(slot_at * TILE, TILE)

    @pl.when(live)
    def _():
        for head in range(HEADS):
            cols = slice(head * head_size, (head + 1) * head_size)
            scores = lax.dot_general(
                q_ref[0, head], kv_ref[0, :, cols], (((1,), (1,)), ((), ())),
                preferred_element_type=jnp.float32,
            )
            s_scr[head, :, pl.ds(key_at, TILE)] = scores * head_size ** (-0.5)
        v_scr[pl.ds(key_at, TILE), :] = kv_ref[0, :, feat_width:]

    @pl.when(jnp.logical_not(live))
    def _():
        v_scr[pl.ds(key_at, TILE), :] = jnp.zeros((TILE, feat_width), v_scr.dtype)

    @pl.when(slot_at == slot_count - 1)
    def _():
        key_slot = lax.broadcasted_iota(jnp.int32, (TILE, slot_count * TILE), 1) // TILE
        key_live = (key_slot >= KT) | (key_slot < live_count)
        for head in range(HEADS):
            cols = slice(head * head_size, (head + 1) * head_size)
            scores = jnp.where(key_live, s_scr[head], -jnp.inf)
            row_max = jnp.max(scores, axis=-1, keepdims=True)
            weights_raw = jnp.exp(scores - row_max)
            probs = (weights_raw / jnp.sum(weights_raw, axis=-1, keepdims=True)).astype(jnp.bfloat16)
            mixed = jnp.dot(probs, v_scr[:, cols], preferred_element_type=jnp.float32)
            o_ref[0, :, cols] = mixed.astype(o_ref.dtype)


def attend(query_tiles, window, slots, counts):
    tile_count, _, feat_width = query_tiles.shape
    slot_count = KT + GLOBAL
    head_size = feat_width // HEADS
    query_heads = query_tiles.reshape(tile_count, TILE, HEADS, head_size).transpose(0, 2, 1, 3)

    def kv_map(i, j, slots_ref, counts_ref):
        live_count = counts_ref[i]
        fetch = jnp.where((j >= KT) | (j < live_count), j, jnp.maximum(live_count - 1, 0))
        return (slots_ref[i, fetch], 0, 0)

    grid_spec = pltpu.PrefetchScalarGridSpec(
        num_scalar_prefetch=2,
        grid=(tile_count, slot_count),
        in_specs=[
            pl.BlockSpec((1, HEADS, TILE, head_size), lambda i, j, s, c: (i, 0, 0, 0)),
            pl.BlockSpec((1, TILE, 2 * feat_width), kv_map),
        ],
        out_specs=pl.BlockSpec((1, TILE, feat_width), lambda i, j, s, c: (i, 0, 0)),
        scratch_shapes=[
            pltpu.VMEM((HEADS, TILE, slot_count * TILE), jnp.float32),
            pltpu.VMEM((slot_count * TILE, feat_width), jnp.bfloat16),
        ],
    )
    return pl.pallas_call(
        attention_kernel,
        grid_spec=grid_spec,
        out_shape=jax.ShapeDtypeStruct(query_tiles.shape, jnp.bfloat16),
        compiler_params=pltpu.CompilerParams(
            dimension_semantics=("arbitrary", "arbitrary"),
        ),
    )(slots, counts, query_heads, window)


def local(
    patches,
    vis_index,
    kv_list,
    kv_count,
    global_tiles,
    frame_table,
    space_table,
    ln_gain,
    ln_bias,
    w_qkv,
    w_out,
):
    tok_rows = patches.shape[0]
    feat_width = patches.shape[1]
    tile_count = tok_rows // TILE
    fsdp_size = lax.axis_size("fsdp")
    seq_size = lax.axis_size("seq")
    seq_at = lax.axis_index("seq")
    group_tiles = tile_count * fsdp_size

    stream = embed(patches, vis_index, frame_table, space_table)

    normed = layer_norm(stream, ln_gain, ln_bias)
    group_rows = lax.all_gather(normed, "fsdp", axis=0, tiled=True).reshape(
        group_tiles, TILE, feat_width
    )
    w_src, group_rows = lax.optimization_barrier((w_qkv, group_rows))
    w_full = gathered_weight(w_src)

    global_ids = global_tiles.astype(jnp.int32)
    global_rows = group_rows[global_ids % group_tiles]
    owners = global_ids // group_tiles
    seq_bits = seq_size.bit_length() - 1
    y_first = [b for b in (1, 2) if b < seq_bits]
    y_first += [b for b in range(seq_bits - 1, -1, -1) if b not in y_first]
    x_first = [b for b in range(seq_bits - 1, -1, -1) if b not in (1, 2)]
    x_first += [b for b in (1, 2) if b < seq_bits]
    halves = []
    for bit_order, part in zip((y_first, x_first), jnp.split(global_rows, 2, axis=2)):
        done_bits = 0
        for bit in bit_order:
            step = 1 << bit
            held = ((seq_at ^ owners) & ~done_bits & (seq_size - 1)) == 0
            done_bits |= step
            got = lax.ppermute(part, "seq", [(i, i ^ step) for i in range(seq_size)])
            part = jnp.where(held[:, None, None], part, got)
        halves.append(part)
    global_rows = jnp.concatenate(halves, axis=2)
    near_blocks = []
    near_rank = []
    for reach in REACH:
        picks, rank = near_tiles(kv_list, seq_at + reach, group_tiles)
        asked = passed_along(picks, "seq", reach)
        near_blocks.append(passed_along(group_rows[asked], "seq", -reach))
        near_rank.append(rank)
    window_rows = jnp.concatenate(
        [group_rows] + near_blocks + [global_rows], axis=0
    )
    window = jnp.dot(
        window_rows.reshape(-1, feat_width), w_full[:, feat_width:],
        preferred_element_type=jnp.float32,
    ).astype(jnp.bfloat16).reshape(-1, TILE, 2 * feat_width)
    query = jnp.dot(
        normed, w_full[:, :feat_width], preferred_element_type=jnp.float32
    ).astype(jnp.bfloat16)
    near_rank = jnp.stack(near_rank)

    entry_group = kv_list // group_tiles
    entry_local = kv_list % group_tiles
    reach_of = entry_group - seq_at
    reach_slot = jnp.where(reach_of < 0, reach_of + 2, reach_of + 1)
    reach_slot = jnp.clip(reach_slot, 0, len(REACH) - 1)
    entry_rank = near_rank[reach_slot, entry_local]
    local_lists = jnp.where(
        reach_of == 0, entry_local, group_tiles + NEAR * reach_slot + jnp.clip(entry_rank, 0, NEAR - 1)
    )
    global_slots = group_tiles + NEAR * len(REACH) + jnp.arange(GLOBAL, dtype=jnp.int32)

    query_tiles = query.reshape(tile_count, TILE, feat_width)
    slots = jnp.concatenate(
        [local_lists, jnp.broadcast_to(global_slots, (tile_count, GLOBAL))], axis=1
    ).astype(jnp.int32)
    heads_out = attend(query_tiles, window, slots, kv_count).reshape(tok_rows, feat_width)
    return jnp.dot(
        heads_out,
        lax.all_gather(w_out, "fsdp", axis=0, tiled=True),
        preferred_element_type=jnp.float32,
    ).astype(jnp.bfloat16)


def solution(mesh):
    return jax.shard_map(
        local,
        mesh=mesh,
        in_specs=(
            P(("seq", "fsdp"), None),
            P(("seq", "fsdp")),
            P(("seq", "fsdp"), None),
            P(("seq", "fsdp")),
            P(),
            P(),
            P(),
            P(),
            P(),
            P("fsdp", None),
            P("fsdp", None),
        ),
        out_specs=P(("seq", "fsdp"), None),
        check_vma=False,
    )
```

```python
import jax
import jax.numpy as jnp
from jax import lax
from jax.experimental import pallas as pl
from jax.experimental.pallas import tpu as pltpu
from jax.sharding import PartitionSpec as P

HEADS = 16
TILE = 128
KT = 16
GLOBAL = 2
PATCHES = 512
NEAR = 3
REACH = (-2, -1, 1, 2)


def passed_along(block, axis, distance):
    devices = range(lax.axis_size(axis))
    route = [(i - distance, i) for i in devices if i - distance in devices]
    return lax.ppermute(block, axis, route)


def gathered_weight(shard):
    core = lax.axis_index("seq") % 2
    half = shard.shape[1] // 2
    mine = lax.all_gather(
        lax.dynamic_slice_in_dim(shard, core * half, half, 1), "fsdp", axis=0, tiled=True
    )
    seq_size = lax.axis_size("seq")
    other = lax.ppermute(mine, "seq", [(i, i ^ 1) for i in range(seq_size)])
    low = jnp.where(core == 0, mine, other)
    high = jnp.where(core == 0, other, mine)
    return jnp.concatenate([low, high], axis=1)


def layer_norm(stream, ln_gain, ln_bias):
    stream32 = stream.astype(jnp.float32)
    mean_val = jnp.mean(stream32, axis=-1, keepdims=True)
    centred = stream32 - mean_val
    variance = jnp.mean(centred * centred, axis=-1, keepdims=True)
    scaled = centred * lax.rsqrt(variance + 1e-06)
    return (scaled * ln_gain.astype(jnp.float32) + ln_bias.astype(jnp.float32)).astype(jnp.bfloat16)


def embed(patches, vis_index, frame_table, space_table):
    frame_ids = vis_index // PATCHES
    patch_ids = vis_index % PATCHES
    return (
        patches.astype(jnp.float32)
        + frame_table[frame_ids].astype(jnp.float32)
        + space_table[patch_ids].astype(jnp.float32)
    ).astype(jnp.bfloat16)


def near_tiles(entries, group, group_tiles):
    cand = group * group_tiles + jnp.arange(group_tiles, dtype=jnp.int32)
    named = jnp.any(entries.reshape(-1, 1) == cand[None, :], axis=0)
    rank = jnp.cumsum(named.astype(jnp.int32)) - 1
    local_ids = jnp.arange(group_tiles, dtype=jnp.int32)
    picks = jnp.stack(
        [jnp.sum(jnp.where(named & (rank == j), local_ids, 0)) for j in range(NEAR)]
    )
    return picks, rank


def attention_kernel(own_ref, rest_ref, src_ref, counts_ref, q_ref, kv_own, kv_rest, o_ref, s_scr, v_scr):
    tile_at = pl.program_id(0)
    slot_at = pl.program_id(1)
    slot_count = KT + GLOBAL
    head_size = q_ref.shape[-1]
    feat_width = head_size * HEADS
    live_count = counts_ref[tile_at]
    live = (slot_at >= KT) | (slot_at < live_count)
    key_at = pl.multiple_of(slot_at * TILE, TILE)

    from_rest = src_ref[tile_at, slot_at] == 1

    def take(kv_ref):
        for head in range(HEADS):
            cols = slice(head * head_size, (head + 1) * head_size)
            scores = lax.dot_general(
                q_ref[0, head], kv_ref[0, :, cols], (((1,), (1,)), ((), ())),
                preferred_element_type=jnp.float32,
            )
            s_scr[head, :, pl.ds(key_at, TILE)] = scores * head_size ** (-0.5)
        v_scr[pl.ds(key_at, TILE), :] = kv_ref[0, :, feat_width:]

    @pl.when(live & jnp.logical_not(from_rest))
    def _():
        take(kv_own)

    @pl.when(live & from_rest)
    def _():
        take(kv_rest)

    @pl.when(jnp.logical_not(live))
    def _():
        v_scr[pl.ds(key_at, TILE), :] = jnp.zeros((TILE, feat_width), v_scr.dtype)

    @pl.when(slot_at == slot_count - 1)
    def _():
        key_slot = lax.broadcasted_iota(jnp.int32, (TILE, slot_count * TILE), 1) // TILE
        key_live = (key_slot >= KT) | (key_slot < live_count)
        for head in range(HEADS):
            cols = slice(head * head_size, (head + 1) * head_size)
            scores = jnp.where(key_live, s_scr[head], -jnp.inf)
            row_max = jnp.max(scores, axis=-1, keepdims=True)
            weights_raw = jnp.exp(scores - row_max)
            probs = (weights_raw / jnp.sum(weights_raw, axis=-1, keepdims=True)).astype(jnp.bfloat16)
            mixed = jnp.dot(probs, v_scr[:, cols], preferred_element_type=jnp.float32)
            o_ref[0, :, cols] = mixed.astype(o_ref.dtype)


def attend(query_tiles, window_own, window_rest, slots, counts):
    tile_count, _, feat_width = query_tiles.shape
    slot_count = KT + GLOBAL
    head_size = feat_width // HEADS
    own_tiles = window_own.shape[0]
    query_heads = query_tiles.reshape(tile_count, TILE, HEADS, head_size).transpose(0, 2, 1, 3)
    own_at = jnp.zeros((tile_count,), jnp.int32)
    rest_at = jnp.zeros((tile_count,), jnp.int32)
    own_cols, rest_cols, src_cols = [], [], []
    for j in range(slot_count):
        live = (j >= KT) | (j < counts)
        use_rest = slots[:, j] >= own_tiles
        own_at = jnp.where(live & ~use_rest, slots[:, j], own_at)
        rest_at = jnp.where(live & use_rest, slots[:, j] - own_tiles, rest_at)
        own_cols.append(own_at)
        rest_cols.append(rest_at)
        src_cols.append(use_rest.astype(jnp.int32))
    own_table = jnp.clip(jnp.stack(own_cols, axis=1), 0, own_tiles - 1)
    rest_table = jnp.clip(jnp.stack(rest_cols, axis=1), 0, window_rest.shape[0] - 1)
    src_table = jnp.stack(src_cols, axis=1)

    grid_spec = pltpu.PrefetchScalarGridSpec(
        num_scalar_prefetch=4,
        grid=(tile_count, slot_count),
        in_specs=[
            pl.BlockSpec((1, HEADS, TILE, head_size), lambda i, j, o, r, s, c: (i, 0, 0, 0)),
            pl.BlockSpec((1, TILE, 2 * feat_width), lambda i, j, o, r, s, c: (o[i, j], 0, 0)),
            pl.BlockSpec((1, TILE, 2 * feat_width), lambda i, j, o, r, s, c: (r[i, j], 0, 0)),
        ],
        out_specs=pl.BlockSpec((1, TILE, feat_width), lambda i, j, o, r, s, c: (i, 0, 0)),
        scratch_shapes=[
            pltpu.VMEM((HEADS, TILE, slot_count * TILE), jnp.float32),
            pltpu.VMEM((slot_count * TILE, feat_width), jnp.bfloat16),
        ],
    )
    return pl.pallas_call(
        attention_kernel,
        grid_spec=grid_spec,
        out_shape=jax.ShapeDtypeStruct(query_tiles.shape, jnp.bfloat16),
        compiler_params=pltpu.CompilerParams(
            dimension_semantics=("arbitrary", "arbitrary"),
        ),
    )(own_table, rest_table, src_table, counts, query_heads, window_own, window_rest)


def local(
    patches,
    vis_index,
    kv_list,
    kv_count,
    global_tiles,
    frame_table,
    space_table,
    ln_gain,
    ln_bias,
    w_qkv,
    w_out,
):
    tok_rows = patches.shape[0]
    feat_width = patches.shape[1]
    tile_count = tok_rows // TILE
    fsdp_size = lax.axis_size("fsdp")
    seq_size = lax.axis_size("seq")
    seq_at = lax.axis_index("seq")
    group_tiles = tile_count * fsdp_size

    stream = embed(patches, vis_index, frame_table, space_table)

    normed = layer_norm(stream, ln_gain, ln_bias)
    group_rows = lax.all_gather(normed, "fsdp", axis=0, tiled=True).reshape(
        group_tiles, TILE, feat_width
    )
    w_src, group_rows = lax.optimization_barrier((w_qkv, group_rows))
    w_full = gathered_weight(w_src)

    global_ids = global_tiles.astype(jnp.int32)
    global_rows = group_rows[global_ids % group_tiles]
    owners = global_ids // group_tiles
    seq_bits = seq_size.bit_length() - 1
    bit_order = [b for b in (1, 2) if b < seq_bits]
    bit_order += [b for b in range(seq_bits - 1, -1, -1) if b not in bit_order]
    done_bits = 0
    for bit in bit_order:
        step = 1 << bit
        held = ((seq_at ^ owners) & ~done_bits & (seq_size - 1)) == 0
        done_bits |= step
        got = lax.ppermute(global_rows, "seq", [(i, i ^ step) for i in range(seq_size)])
        global_rows = jnp.where(held[:, None, None], global_rows, got)
    near_blocks = []
    near_rank = []
    for reach in REACH:
        picks, rank = near_tiles(kv_list, seq_at + reach, group_tiles)
        asked = passed_along(picks, "seq", reach)
        near_blocks.append(passed_along(group_rows[asked], "seq", -reach))
        near_rank.append(rank)
    def project(rows):
        return jnp.dot(
            rows.reshape(-1, feat_width), w_full[:, feat_width:],
            preferred_element_type=jnp.float32,
        ).astype(jnp.bfloat16).reshape(-1, TILE, 2 * feat_width)

    window_own = project(group_rows)
    window_rest = project(jnp.concatenate(near_blocks + [global_rows], axis=0))
    query = jnp.dot(
        normed, w_full[:, :feat_width], preferred_element_type=jnp.float32
    ).astype(jnp.bfloat16)
    near_rank = jnp.stack(near_rank)

    entry_group = kv_list // group_tiles
    entry_local = kv_list % group_tiles
    reach_of = entry_group - seq_at
    reach_slot = jnp.where(reach_of < 0, reach_of + 2, reach_of + 1)
    reach_slot = jnp.clip(reach_slot, 0, len(REACH) - 1)
    entry_rank = near_rank[reach_slot, entry_local]
    local_lists = jnp.where(
        reach_of == 0, entry_local, group_tiles + NEAR * reach_slot + jnp.clip(entry_rank, 0, NEAR - 1)
    )
    global_slots = group_tiles + NEAR * len(REACH) + jnp.arange(GLOBAL, dtype=jnp.int32)

    query_tiles = query.reshape(tile_count, TILE, feat_width)
    slots = jnp.concatenate(
        [local_lists, jnp.broadcast_to(global_slots, (tile_count, GLOBAL))], axis=1
    ).astype(jnp.int32)
    heads_out = attend(query_tiles, window_own, window_rest, slots, kv_count).reshape(tok_rows, feat_width)
    return jnp.dot(
        heads_out,
        lax.all_gather(w_out, "fsdp", axis=0, tiled=True),
        preferred_element_type=jnp.float32,
    ).astype(jnp.bfloat16)


def solution(mesh):
    return jax.shard_map(
        local,
        mesh=mesh,
        in_specs=(
            P(("seq", "fsdp"), None),
            P(("seq", "fsdp")),
            P(("seq", "fsdp"), None),
            P(("seq", "fsdp")),
            P(),
            P(),
            P(),
            P(),
            P(),
            P("fsdp", None),
            P("fsdp", None),
        ),
        out_specs=P(("seq", "fsdp"), None),
        check_vma=False,
    )
```

```python
import jax
import jax.numpy as jnp
from jax import lax
from jax.experimental import pallas as pl
from jax.experimental.pallas import tpu as pltpu
from jax.sharding import PartitionSpec as P

HEADS = 16
TILE = 128
KT = 16
GLOBAL = 2
PATCHES = 512
NEAR = 3
REACH = (-2, -1, 1, 2)


def passed_along(block, axis, distance):
    devices = range(lax.axis_size(axis))
    route = [(i - distance, i) for i in devices if i - distance in devices]
    return lax.ppermute(block, axis, route)


def gathered_weight(shard):
    core = lax.axis_index("seq") % 2
    half = shard.shape[1] // 2
    mine = lax.all_gather(
        lax.dynamic_slice_in_dim(shard, core * half, half, 1), "fsdp", axis=0, tiled=True
    )
    seq_size = lax.axis_size("seq")
    other = lax.ppermute(mine, "seq", [(i, i ^ 1) for i in range(seq_size)])
    low = jnp.where(core == 0, mine, other)
    high = jnp.where(core == 0, other, mine)
    return jnp.concatenate([low, high], axis=1)


def layer_norm(stream, ln_gain, ln_bias):
    stream32 = stream.astype(jnp.float32)
    mean_val = jnp.mean(stream32, axis=-1, keepdims=True)
    centred = stream32 - mean_val
    variance = jnp.mean(centred * centred, axis=-1, keepdims=True)
    scaled = centred * lax.rsqrt(variance + 1e-06)
    return (scaled * ln_gain.astype(jnp.float32) + ln_bias.astype(jnp.float32)).astype(jnp.bfloat16)


def embed(patches, vis_index, frame_table, space_table):
    frame_ids = vis_index // PATCHES
    patch_ids = vis_index % PATCHES
    return (
        patches.astype(jnp.float32)
        + frame_table[frame_ids].astype(jnp.float32)
        + space_table[patch_ids].astype(jnp.float32)
    ).astype(jnp.bfloat16)


def near_tiles(entries, group, group_tiles):
    cand = group * group_tiles + jnp.arange(group_tiles, dtype=jnp.int32)
    named = jnp.any(entries.reshape(-1, 1) == cand[None, :], axis=0)
    rank = jnp.cumsum(named.astype(jnp.int32)) - 1
    local_ids = jnp.arange(group_tiles, dtype=jnp.int32)
    picks = jnp.stack(
        [jnp.sum(jnp.where(named & (rank == j), local_ids, 0)) for j in range(NEAR)]
    )
    return picks, rank


def attention_kernel(slots_ref, counts_ref, q_ref, kv_ref, o_ref, s_scr, v_scr):
    tile_at = pl.program_id(0)
    slot_at = pl.program_id(1)
    slot_count = KT + GLOBAL
    feat_width = q_ref.shape[-1]
    head_size = feat_width // HEADS
    live_count = counts_ref[tile_at]
    live = (slot_at >= KT) | (slot_at < live_count)
    key_at = pl.multiple_of(slot_at * TILE, TILE)

    @pl.when(live)
    def _():
        for head in range(HEADS):
            cols = slice(head * head_size, (head + 1) * head_size)
            scores = lax.dot_general(
                q_ref[0, :, cols], kv_ref[0, :, cols], (((1,), (1,)), ((), ())),
                preferred_element_type=jnp.float32,
            )
            s_scr[head, :, pl.ds(key_at, TILE)] = scores * head_size ** (-0.5)
        v_scr[pl.ds(key_at, TILE), :] = kv_ref[0, :, feat_width:]

    @pl.when(jnp.logical_not(live))
    def _():
        v_scr[pl.ds(key_at, TILE), :] = jnp.zeros((TILE, feat_width), v_scr.dtype)

    @pl.when(slot_at == slot_count - 1)
    def _():
        key_slot = lax.broadcasted_iota(jnp.int32, (TILE, slot_count * TILE), 1) // TILE
        key_live = (key_slot >= KT) | (key_slot < live_count)
        for head in range(HEADS):
            cols = slice(head * head_size, (head + 1) * head_size)
            scores = jnp.where(key_live, s_scr[head], -jnp.inf)
            row_max = jnp.max(scores, axis=-1, keepdims=True)
            weights_raw = jnp.exp(scores - row_max)
            probs = (weights_raw / jnp.sum(weights_raw, axis=-1, keepdims=True)).astype(jnp.bfloat16)
            mixed = jnp.dot(probs, v_scr[:, cols], preferred_element_type=jnp.float32)
            o_ref[0, :, cols] = mixed.astype(o_ref.dtype)


def attend(query_tiles, window, slots, counts):
    tile_count, _, feat_width = query_tiles.shape
    slot_count = KT + GLOBAL

    def kv_map(i, j, slots_ref, counts_ref):
        live_count = counts_ref[i]
        fetch = jnp.where((j >= KT) | (j < live_count), j, jnp.maximum(live_count - 1, 0))
        return (slots_ref[i, fetch], 0, 0)

    grid_spec = pltpu.PrefetchScalarGridSpec(
        num_scalar_prefetch=2,
        grid=(tile_count, slot_count),
        in_specs=[
            pl.BlockSpec((1, TILE, feat_width), lambda i, j, s, c: (i, 0, 0)),
            pl.BlockSpec((1, TILE, 2 * feat_width), kv_map),
        ],
        out_specs=pl.BlockSpec((1, TILE, feat_width), lambda i, j, s, c: (i, 0, 0)),
        scratch_shapes=[
            pltpu.VMEM((HEADS, TILE, slot_count * TILE), jnp.float32),
            pltpu.VMEM((slot_count * TILE, feat_width), jnp.bfloat16),
        ],
    )
    return pl.pallas_call(
        attention_kernel,
        grid_spec=grid_spec,
        out_shape=jax.ShapeDtypeStruct(query_tiles.shape, jnp.bfloat16),
        compiler_params=pltpu.CompilerParams(
            dimension_semantics=("arbitrary", "arbitrary"),
        ),
    )(slots, counts, query_tiles, window)


def local(
    patches,
    vis_index,
    kv_list,
    kv_count,
    global_tiles,
    frame_table,
    space_table,
    ln_gain,
    ln_bias,
    w_qkv,
    w_out,
):
    tok_rows = patches.shape[0]
    feat_width = patches.shape[1]
    tile_count = tok_rows // TILE
    fsdp_size = lax.axis_size("fsdp")
    seq_size = lax.axis_size("seq")
    seq_at = lax.axis_index("seq")
    group_tiles = tile_count * fsdp_size

    stream = embed(patches, vis_index, frame_table, space_table)

    normed = layer_norm(stream, ln_gain, ln_bias)
    group_rows = lax.all_gather(normed, "fsdp", axis=0, tiled=True).reshape(
        group_tiles, TILE, feat_width
    )
    w_src, group_rows = lax.optimization_barrier((w_qkv, group_rows))
    w_full = gathered_weight(w_src)

    global_ids = global_tiles.astype(jnp.int32)
    global_rows = group_rows[global_ids % group_tiles]
    owners = global_ids // group_tiles
    seq_bits = seq_size.bit_length() - 1
    bit_order = [b for b in (0, 1, 2) if b < seq_bits]
    bit_order += [b for b in range(seq_bits - 1, -1, -1) if b not in bit_order]
    done_bits = 0
    for bit in bit_order:
        step = 1 << bit
        held = ((seq_at ^ owners) & ~done_bits & (seq_size - 1)) == 0
        done_bits |= step
        got = lax.ppermute(global_rows, "seq", [(i, i ^ step) for i in range(seq_size)])
        global_rows = jnp.where(held[:, None, None], global_rows, got)
    near_blocks = []
    near_rank = []
    for reach in REACH:
        picks, rank = near_tiles(kv_list, seq_at + reach, group_tiles)
        asked = passed_along(picks, "seq", reach)
        near_blocks.append(passed_along(group_rows[asked], "seq", -reach))
        near_rank.append(rank)
    window_rows = jnp.concatenate(
        [group_rows] + near_blocks + [global_rows], axis=0
    )
    window = jnp.dot(
        window_rows.reshape(-1, feat_width), w_full[:, feat_width:],
        preferred_element_type=jnp.float32,
    ).astype(jnp.bfloat16).reshape(-1, TILE, 2 * feat_width)
    query = jnp.dot(
        normed, w_full[:, :feat_width], preferred_element_type=jnp.float32
    ).astype(jnp.bfloat16)
    near_rank = jnp.stack(near_rank)

    entry_group = kv_list // group_tiles
    entry_local = kv_list % group_tiles
    reach_of = entry_group - seq_at
    reach_slot = jnp.where(reach_of < 0, reach_of + 2, reach_of + 1)
    reach_slot = jnp.clip(reach_slot, 0, len(REACH) - 1)
    entry_rank = near_rank[reach_slot, entry_local]
    local_lists = jnp.where(
        reach_of == 0, entry_local, group_tiles + NEAR * reach_slot + jnp.clip(entry_rank, 0, NEAR - 1)
    )
    global_slots = group_tiles + NEAR * len(REACH) + jnp.arange(GLOBAL, dtype=jnp.int32)

    query_tiles = query.reshape(tile_count, TILE, feat_width)
    slots = jnp.concatenate(
        [local_lists, jnp.broadcast_to(global_slots, (tile_count, GLOBAL))], axis=1
    ).astype(jnp.int32)
    heads_out = attend(query_tiles, window, slots, kv_count).reshape(tok_rows, feat_width)
    return jnp.dot(
        heads_out,
        lax.all_gather(w_out, "fsdp", axis=0, tiled=True),
        preferred_element_type=jnp.float32,
    ).astype(jnp.bfloat16)


def solution(mesh):
    return jax.shard_map(
        local,
        mesh=mesh,
        in_specs=(
            P(("seq", "fsdp"), None),
            P(("seq", "fsdp")),
            P(("seq", "fsdp"), None),
            P(("seq", "fsdp")),
            P(),
            P(),
            P(),
            P(),
            P(),
            P("fsdp", None),
            P("fsdp", None),
        ),
        out_specs=P(("seq", "fsdp"), None),
        check_vma=False,
    )
```

```python
import jax
import jax.numpy as jnp
from jax import lax
from jax.experimental import pallas as pl
from jax.experimental.pallas import tpu as pltpu
from jax.sharding import PartitionSpec as P

HEADS = 16
TILE = 128
KT = 16
GLOBAL = 2
PATCHES = 512
NEAR = 3
REACH = (-2, -1, 1, 2)


def passed_along(block, axis, distance):
    devices = range(lax.axis_size(axis))
    route = [(i - distance, i) for i in devices if i - distance in devices]
    return lax.ppermute(block, axis, route)


def gathered_weight(shard):
    core = lax.axis_index("seq") % 2
    half = shard.shape[1] // 2
    mine = lax.all_gather(
        lax.dynamic_slice_in_dim(shard, core * half, half, 1), "fsdp", axis=0, tiled=True
    )
    seq_size = lax.axis_size("seq")
    other = lax.ppermute(mine, "seq", [(i, i ^ 1) for i in range(seq_size)])
    low = jnp.where(core == 0, mine, other)
    high = jnp.where(core == 0, other, mine)
    return jnp.concatenate([low, high], axis=1)


def layer_norm(stream, ln_gain, ln_bias):
    stream32 = stream.astype(jnp.float32)
    mean_val = jnp.mean(stream32, axis=-1, keepdims=True)
    centred = stream32 - mean_val
    variance = jnp.mean(centred * centred, axis=-1, keepdims=True)
    scaled = centred * lax.rsqrt(variance + 1e-06)
    return (scaled * ln_gain.astype(jnp.float32) + ln_bias.astype(jnp.float32)).astype(jnp.bfloat16)


def embed(patches, vis_index, frame_table, space_table):
    frame_ids = vis_index // PATCHES
    patch_ids = vis_index % PATCHES
    return (
        patches.astype(jnp.float32)
        + frame_table[frame_ids].astype(jnp.float32)
        + space_table[patch_ids].astype(jnp.float32)
    ).astype(jnp.bfloat16)


def near_tiles(entries, group, group_tiles):
    cand = group * group_tiles + jnp.arange(group_tiles, dtype=jnp.int32)
    named = jnp.any(entries.reshape(-1, 1) == cand[None, :], axis=0)
    rank = jnp.cumsum(named.astype(jnp.int32)) - 1
    local_ids = jnp.arange(group_tiles, dtype=jnp.int32)
    picks = jnp.stack(
        [jnp.sum(jnp.where(named & (rank == j), local_ids, 0)) for j in range(NEAR)]
    )
    return picks, rank


def attention_kernel(slots_ref, counts_ref, q_ref, kv_ref, o_ref, s_scr, v_scr):
    tile_at = pl.program_id(0)
    slot_at = pl.program_id(1)
    slot_count = KT + GLOBAL
    feat_width = q_ref.shape[-1]
    head_size = feat_width // HEADS
    live_count = counts_ref[tile_at]
    live = (slot_at >= KT) | (slot_at < live_count)
    key_at = pl.multiple_of(slot_at * TILE, TILE)

    @pl.when(live)
    def _():
        for head in range(HEADS):
            cols = slice(head * head_size, (head + 1) * head_size)
            scores = lax.dot_general(
                q_ref[0, :, cols], kv_ref[0, :, cols], (((1,), (1,)), ((), ())),
                preferred_element_type=jnp.float32,
            )
            s_scr[head, :, pl.ds(key_at, TILE)] = scores * head_size ** (-0.5)
        v_scr[pl.ds(key_at, TILE), :] = kv_ref[0, :, feat_width:]

    @pl.when(jnp.logical_not(live))
    def _():
        v_scr[pl.ds(key_at, TILE), :] = jnp.zeros((TILE, feat_width), v_scr.dtype)

    @pl.when(slot_at == slot_count - 1)
    def _():
        key_slot = lax.broadcasted_iota(jnp.int32, (TILE, slot_count * TILE), 1) // TILE
        key_live = (key_slot >= KT) | (key_slot < live_count)
        for head in range(HEADS):
            cols = slice(head * head_size, (head + 1) * head_size)
            scores = jnp.where(key_live, s_scr[head], -jnp.inf)
            row_max = jnp.max(scores, axis=-1, keepdims=True)
            weights_raw = jnp.exp(scores - row_max)
            probs = (weights_raw / jnp.sum(weights_raw, axis=-1, keepdims=True)).astype(jnp.bfloat16)
            mixed = jnp.dot(probs, v_scr[:, cols], preferred_element_type=jnp.float32)
            o_ref[0, :, cols] = mixed.astype(o_ref.dtype)


def attend(query_tiles, window, slots, counts):
    tile_count, _, feat_width = query_tiles.shape
    slot_count = KT + GLOBAL

    def kv_map(i, j, slots_ref, counts_ref):
        live_count = counts_ref[i]
        fetch = jnp.where((j >= KT) | (j < live_count), j, jnp.maximum(live_count - 1, 0))
        return (slots_ref[i, fetch], 0, 0)

    grid_spec = pltpu.PrefetchScalarGridSpec(
        num_scalar_prefetch=2,
        grid=(tile_count, slot_count),
        in_specs=[
            pl.BlockSpec((1, TILE, feat_width), lambda i, j, s, c: (i, 0, 0)),
            pl.BlockSpec((1, TILE, 2 * feat_width), kv_map),
        ],
        out_specs=pl.BlockSpec((1, TILE, feat_width), lambda i, j, s, c: (i, 0, 0)),
        scratch_shapes=[
            pltpu.VMEM((HEADS, TILE, slot_count * TILE), jnp.float32),
            pltpu.VMEM((slot_count * TILE, feat_width), jnp.bfloat16),
        ],
    )
    return pl.pallas_call(
        attention_kernel,
        grid_spec=grid_spec,
        out_shape=jax.ShapeDtypeStruct(query_tiles.shape, jnp.bfloat16),
        compiler_params=pltpu.CompilerParams(
            dimension_semantics=("arbitrary", "arbitrary"),
        ),
    )(slots, counts, query_tiles, window)


def local(
    patches,
    vis_index,
    kv_list,
    kv_count,
    global_tiles,
    frame_table,
    space_table,
    ln_gain,
    ln_bias,
    w_qkv,
    w_out,
):
    tok_rows = patches.shape[0]
    feat_width = patches.shape[1]
    tile_count = tok_rows // TILE
    fsdp_size = lax.axis_size("fsdp")
    seq_size = lax.axis_size("seq")
    seq_at = lax.axis_index("seq")
    group_tiles = tile_count * fsdp_size

    stream = embed(patches, vis_index, frame_table, space_table)

    normed = layer_norm(stream, ln_gain, ln_bias)
    group_rows = lax.all_gather(normed, "fsdp", axis=0, tiled=True).reshape(
        group_tiles, TILE, feat_width
    )
    w_src, group_rows = lax.optimization_barrier((w_qkv, group_rows))
    w_full = gathered_weight(w_src)

    global_ids = global_tiles.astype(jnp.int32)
    global_rows = group_rows[global_ids % group_tiles]
    owners = global_ids // group_tiles
    seq_bits = seq_size.bit_length() - 1
    bit_order = [b for b in (2, 1) if b < seq_bits]
    bit_order += [b for b in range(seq_bits - 1, -1, -1) if b not in bit_order]
    done_bits = 0
    for bit in bit_order:
        step = 1 << bit
        held = ((seq_at ^ owners) & ~done_bits & (seq_size - 1)) == 0
        done_bits |= step
        got = lax.ppermute(global_rows, "seq", [(i, i ^ step) for i in range(seq_size)])
        global_rows = jnp.where(held[:, None, None], global_rows, got)
    near_blocks = []
    near_rank = []
    for reach in REACH:
        picks, rank = near_tiles(kv_list, seq_at + reach, group_tiles)
        asked = passed_along(picks, "seq", reach)
        near_blocks.append(passed_along(group_rows[asked], "seq", -reach))
        near_rank.append(rank)
    window_rows = jnp.concatenate(
        [group_rows] + near_blocks + [global_rows], axis=0
    )
    window = jnp.dot(
        window_rows.reshape(-1, feat_width), w_full[:, feat_width:],
        preferred_element_type=jnp.float32,
    ).astype(jnp.bfloat16).reshape(-1, TILE, 2 * feat_width)
    query = jnp.dot(
        normed, w_full[:, :feat_width], preferred_element_type=jnp.float32
    ).astype(jnp.bfloat16)
    near_rank = jnp.stack(near_rank)

    entry_group = kv_list // group_tiles
    entry_local = kv_list % group_tiles
    reach_of = entry_group - seq_at
    reach_slot = jnp.where(reach_of < 0, reach_of + 2, reach_of + 1)
    reach_slot = jnp.clip(reach_slot, 0, len(REACH) - 1)
    entry_rank = near_rank[reach_slot, entry_local]
    local_lists = jnp.where(
        reach_of == 0, entry_local, group_tiles + NEAR * reach_slot + jnp.clip(entry_rank, 0, NEAR - 1)
    )
    global_slots = group_tiles + NEAR * len(REACH) + jnp.arange(GLOBAL, dtype=jnp.int32)

    query_tiles = query.reshape(tile_count, TILE, feat_width)
    slots = jnp.concatenate(
        [local_lists, jnp.broadcast_to(global_slots, (tile_count, GLOBAL))], axis=1
    ).astype(jnp.int32)
    heads_out = attend(query_tiles, window, slots, kv_count).reshape(tok_rows, feat_width)
    return jnp.dot(
        heads_out,
        lax.all_gather(w_out, "fsdp", axis=0, tiled=True),
        preferred_element_type=jnp.float32,
    ).astype(jnp.bfloat16)


def solution(mesh):
    return jax.shard_map(
        local,
        mesh=mesh,
        in_specs=(
            P(("seq", "fsdp"), None),
            P(("seq", "fsdp")),
            P(("seq", "fsdp"), None),
            P(("seq", "fsdp")),
            P(),
            P(),
            P(),
            P(),
            P(),
            P("fsdp", None),
            P("fsdp", None),
        ),
        out_specs=P(("seq", "fsdp"), None),
        check_vma=False,
    )
```
